128 devices in a mesh: seq: 32 (over y, z, core), tp: 4 (over x).
Axes of the slice: x: 4, y: 4, z: 4, core: 2. Of those that a mesh axis runs over, the one named last changes fastest.
Arguments:
- query_rows: bfloat16 [16384, 2560], P(('seq', 'tp')), may hold values from -6 to 6
- key_rows: bfloat16 [16384, 512], P(('seq', 'tp')), may hold values from -6 to 6
- value_rows: bfloat16 [16384, 512], P(('seq', 'tp')), may hold values from -6 to 6
- out_grad: bfloat16 [16384, 2560], P(('seq', 'tp')), may hold values from -6 to 6
- doc_lengths: int32 [8], replicated, may hold values from 1 to 4096, as said below
Outputs:
- attended: bfloat16 [16384, 2560], P(('seq', 'tp'))
- query_grad: bfloat16 [16384, 2560], P(('seq', 'tp'))
- key_grad: bfloat16 [16384, 512], P(('seq', 'tp'))
- value_grad: bfloat16 [16384, 512], P(('seq', 'tp'))
The draws below stay inside these ranges and needn't reach their ends.
Inputs may be any that keep to these rules, and one draw needn't show every extreme that they name: `doc_lengths`: 8 document lengths in token order that sum to 16384; exactly one of them is 4096, all others are shorter.
All inputs are finite; a program needn't handle non-finite values.
Results may differ from the reference program's by a relative error of at most 0.022.
Values may be sent and summed in bfloat16 or wider, within the bound.
No kernel may reach another device: no remote copies, remote signals or barrier semaphores. Data moves between devices by JAX's collectives and lax.ppermute only.
A program may use at most 64 MiB of HBM per device.

```python
import math
import jax
import jax.numpy as jnp
from jax import lax

HD = 128
QH = 20
KVH = 4
DOCS = 8
TOKENS = 16384
LONG = 4096


def doc_plan(key):
    base = jax.random.fold_in(key, 11)
    first, second = jax.random.split(base)
    remainder = TOKENS - LONG
    pieces = DOCS - 1
    share = remainder // pieces
    pairs = pieces // 2
    moves = jax.random.randint(first, (pairs,), 1 - share, share).astype(jnp.int32)
    paired = jnp.stack([share + moves, share - moves], axis=1).reshape(2 * pairs)
    shorter = jnp.concatenate([paired, jnp.full((pieces - 2 * pairs,), share, jnp.int32)])
    shorter = shorter.at[pieces - 1].add(remainder - share * pieces)
    long_slot = jax.random.randint(second, (), 0, DOCS)
    ordinal = jnp.arange(DOCS, dtype=jnp.int32)
    source = jnp.clip(ordinal - (ordinal > long_slot).astype(jnp.int32), 0, DOCS - 2)
    lengths = jnp.where(ordinal == long_slot, LONG, shorter[source]).astype(jnp.int32)
    return lengths


def rough_rows(key, shape):
    values_out = jax.random.normal(key, shape, jnp.float32) * 1.6
    return jnp.clip(values_out, -6.0, 6.0)


def draw_doc_lengths(key, part):
    return doc_plan(key)


def draw_key_rows(key, part):
    rows_out = rough_rows(jax.random.fold_in(key, 31), (TOKENS, KVH * HD))
    return rows_out.astype(jnp.bfloat16)


def draw_query_rows(key, part):
    rows_out = rough_rows(jax.random.fold_in(key, 37), (TOKENS, QH * HD))
    return rows_out.astype(jnp.bfloat16)


def steps_of(stream_key, extent, cuts, low, high):
    def one(axis_at, blocks):
        heights = jax.random.uniform(jax.random.fold_in(jax.random.fold_in(stream_key, 6), axis_at), (blocks,), jnp.float32, low / len(cuts), high / len(cuts))
        return jnp.repeat(jnp.exp(heights), extent[axis_at] // blocks).reshape((-1,) + (1,) * (len(extent) - axis_at - 1))

    loudness = one(*cuts[0])
    for cut in cuts[1:]:
        loudness = loudness * one(*cut)
    return loudness


def gaussian(stream_key, extent, deviation, most, cuts=(), kind=jnp.bfloat16):
    values = jax.random.normal(stream_key, extent, jnp.float32) * deviation
    if len(cuts) > 0:
        values = steps_of(stream_key, extent, cuts, -0.22, 0.18) * values
    return jnp.clip(values, min=-most, max=most).astype(kind)


def setup_inputs(seed: int = 0) -> dict:
    streams_of = jax.random.split(jax.random.key(seed), 6)
    query_rows = draw_query_rows(jax.random.fold_in(streams_of[5], 71), 0)
    key_rows = draw_key_rows(jax.random.fold_in(streams_of[5], 71), 0)
    value_rows = gaussian(streams_of[2], (TOKENS, KVH * HD), 1.0, 6.0, ((0, 128),))
    out_grad = gaussian(streams_of[3], (TOKENS, QH * HD), 1.0, 6.0, ((0, 128),))
    doc_lengths = draw_doc_lengths(jax.random.fold_in(streams_of[5], 71), 0)
    return {"query_rows": query_rows, "key_rows": key_rows, "value_rows": value_rows, "out_grad": out_grad, "doc_lengths": doc_lengths}


def reference(query_rows, key_rows, value_rows, out_grad, doc_lengths):
    per_kv = QH // KVH
    scaling = HD ** -0.5
    doc_ends = jnp.cumsum(doc_lengths).astype(jnp.int32)
    positions = jnp.arange(TOKENS, dtype=jnp.int32)
    segments = jnp.sum((positions[:, None] >= doc_ends[None, :]).astype(jnp.int32), axis=1).astype(jnp.int32)
    keys_wide = key_rows.reshape(TOKENS, KVH, HD).astype(jnp.float32)
    values_wide = value_rows.reshape(TOKENS, KVH, HD).astype(jnp.float32)
    block_rows = math.gcd(TOKENS, 512)
    block_count = TOKENS // block_rows
    window = min(TOKENS, LONG + block_rows)

    def window_start(first_row):
        return jnp.clip(first_row + block_rows - window, 0, TOKENS - window).astype(jnp.int32)

    def visible_block(first_row, key_start):
        query_pos = first_row + jnp.arange(block_rows, dtype=jnp.int32)
        query_seg = lax.dynamic_slice_in_dim(segments, first_row, block_rows, 0)
        key_pos = key_start + jnp.arange(window, dtype=jnp.int32)
        key_seg = lax.dynamic_slice_in_dim(segments, key_start, window, 0)
        visible = (key_pos[None, :] <= query_pos[:, None]) & (key_seg[None, :] == query_seg[:, None])
        return visible[:, None, None, :]

    def query_block_of(first_row):
        picked = lax.dynamic_slice_in_dim(query_rows, first_row, block_rows, 0)
        return picked.reshape(block_rows, KVH, per_kv, HD).astype(jnp.float32)

    def forward_block(block_index):
        first_row = (block_index * block_rows).astype(jnp.int32)
        key_start = window_start(first_row)
        spread = visible_block(first_row, key_start)
        keys_near = lax.dynamic_slice_in_dim(keys_wide, key_start, window, 0)
        values_near = lax.dynamic_slice_in_dim(values_wide, key_start, window, 0)
        scores = jnp.einsum("bkgd,tkd->bkgt", query_block_of(first_row), keys_near) * scaling
        scores = jnp.where(spread, scores, -1e30)
        largest = jnp.max(scores, axis=-1)
        weight = jnp.where(spread, jnp.exp(scores - largest[..., None]), 0.0)
        denominator = jnp.sum(weight, axis=-1)
        rounded = lax.optimization_barrier(weight.astype(jnp.bfloat16)).astype(jnp.float32)
        mixed = jnp.einsum("bkgt,tkd->bkgd", rounded, values_near) / denominator[..., None]
        return mixed.astype(jnp.bfloat16).reshape(block_rows, QH * HD), largest + jnp.log(denominator)

    out_blocks, log_blocks = lax.map(forward_block, jnp.arange(block_count, dtype=jnp.int32))
    attended = out_blocks.reshape(TOKENS, QH * HD)
    log_total = log_blocks.reshape(TOKENS, KVH, per_kv)
    grad_wide = out_grad.reshape(TOKENS, KVH, per_kv, HD).astype(jnp.float32)
    row_dot = jnp.sum(grad_wide * attended.reshape(TOKENS, KVH, per_kv, HD).astype(jnp.float32), axis=-1)

    def backward_block(carried, block_index):
        key_sum, value_sum = carried
        first_row = (block_index * block_rows).astype(jnp.int32)
        key_start = window_start(first_row)
        spread = visible_block(first_row, key_start)
        keys_near = lax.dynamic_slice_in_dim(keys_wide, key_start, window, 0)
        values_near = lax.dynamic_slice_in_dim(values_wide, key_start, window, 0)
        query_block = query_block_of(first_row)
        scores = jnp.einsum("bkgd,tkd->bkgt", query_block, keys_near) * scaling
        scores = jnp.where(spread, scores, -1e30)
        log_block = lax.dynamic_slice_in_dim(log_total, first_row, block_rows, 0)
        row_block = lax.dynamic_slice_in_dim(row_dot, first_row, block_rows, 0)
        grad_block = lax.dynamic_slice_in_dim(grad_wide, first_row, block_rows, 0)
        probability = jnp.where(spread, jnp.exp(scores - log_block[..., None]), 0.0)
        prob_rounded = lax.optimization_barrier(probability.astype(jnp.bfloat16)).astype(jnp.float32)
        value_part = jnp.einsum("bkgt,bkgd->tkd", prob_rounded, grad_block)
        grad_prob = jnp.einsum("bkgd,tkd->bkgt", grad_block, values_near)
        grad_score = probability * (grad_prob - row_block[..., None])
        grad_score = lax.optimization_barrier(grad_score.astype(jnp.bfloat16)).astype(jnp.float32)
        query_part = jnp.einsum("bkgt,tkd->bkgd", grad_score, keys_near) * scaling
        key_part = jnp.einsum("bkgt,bkgd->tkd", grad_score, query_block) * scaling
        key_now = lax.dynamic_slice_in_dim(key_sum, key_start, window, 0)
        value_now = lax.dynamic_slice_in_dim(value_sum, key_start, window, 0)
        key_sum = lax.dynamic_update_slice_in_dim(key_sum, key_now + key_part, key_start, 0)
        value_sum = lax.dynamic_update_slice_in_dim(value_sum, value_now + value_part, key_start, 0)
        return (key_sum, value_sum), query_part.astype(jnp.bfloat16).reshape(block_rows, QH * HD)

    zero_sums = jnp.zeros((TOKENS, KVH, HD), jnp.float32)
    (key_sum, value_sum), query_blocks = lax.scan(backward_block, (zero_sums, zero_sums), jnp.arange(block_count, dtype=jnp.int32))
    query_grad = query_blocks.reshape(TOKENS, QH * HD)
    key_grad = key_sum.astype(jnp.bfloat16).reshape(TOKENS, KVH * HD)
    value_grad = value_sum.astype(jnp.bfloat16).reshape(TOKENS, KVH * HD)
    return (attended, query_grad, key_grad, value_grad)
```

```python
import math

import jax
import jax.numpy as jnp
from jax import lax
from jax.sharding import PartitionSpec as P

HD = 128
QH = 20
KVH = 4
LONG = 4096


def shifted(value, axis, by):
    peers = lax.axis_size(axis)
    pairs = [(i, i + by) for i in range(peers) if 0 <= i + by < peers]
    return lax.ppermute(value, axis, pairs)


def segment_of(position, doc_ends):
    return jnp.sum((position >= doc_ends).astype(jnp.int32))


def placed(first_row, row_count, doc_ends):
    position = first_row + jnp.arange(row_count, dtype=jnp.int32)
    segment = jnp.sum((position[:, None] >= doc_ends[None, :]).astype(jnp.int32), axis=1)
    return (position, segment)


def allowed(query_pos, query_seg, key_pos, key_seg):
    return (
        (key_pos[None, :] <= query_pos[:, None])
        & (key_pos[None, :] >= 0)
        & (key_seg[None, :] == query_seg[:, None])
    )


def absorb(softmax_state, query_heads, key_block, value_block, visible, scaling):
    running, denominator, accumulated = softmax_state
    scores = (
        jnp.einsum("bkgd,tkd->bkgt", query_heads, key_block, preferred_element_type=jnp.float32)
        * scaling
    )
    spread = visible[:, None, None, :]
    scores = jnp.where(spread, scores, -1e30)
    newest = jnp.maximum(running, jnp.max(scores, axis=-1))
    weight = jnp.where(spread, jnp.exp(scores - newest[..., None]), 0.0)
    shrink = jnp.exp(running - newest)
    denominator = denominator * shrink + jnp.sum(weight, axis=-1)
    accumulated = accumulated * shrink[..., None] + jnp.einsum(
        "bkgt,tkd->bkgd",
        weight.astype(jnp.bfloat16),
        value_block,
        preferred_element_type=jnp.float32,
    )
    return (newest, denominator, accumulated)


def contrib(query_heads, grad_heads, log_total, row_dot, key_block, value_block, visible, scaling):
    scores = (
        jnp.einsum("bkgd,tkd->bkgt", query_heads, key_block, preferred_element_type=jnp.float32)
        * scaling
    )
    spread = visible[:, None, None, :]
    scores = jnp.where(spread, scores, -1e30)
    probability = jnp.where(spread, jnp.exp(scores - log_total[..., None]), 0.0)
    value_part = jnp.einsum(
        "bkgt,bkgd->tkd",
        probability.astype(jnp.bfloat16),
        grad_heads,
        preferred_element_type=jnp.float32,
    )
    grad_prob = jnp.einsum(
        "bkgd,tkd->bkgt", grad_heads, value_block, preferred_element_type=jnp.float32
    )
    grad_score = (probability * (grad_prob - row_dot[..., None])).astype(jnp.bfloat16)
    query_part = (
        jnp.einsum("bkgt,tkd->bkgd", grad_score, key_block, preferred_element_type=jnp.float32)
        * scaling
    )
    key_part = (
        jnp.einsum("bkgt,bkgd->tkd", grad_score, query_heads, preferred_element_type=jnp.float32)
        * scaling
    )
    return (query_part, key_part, value_part)


def per_device(query_rows, key_rows, value_rows, out_grad, doc_lengths):
    per_kv = QH // KVH
    scaling = HD ** (-0.5)
    query_here, key_here, value_here, grad_here = (
        lax.all_to_all(query_rows, "tp", split_axis=1, concat_axis=0, tiled=True),
        lax.all_to_all(key_rows, "tp", split_axis=1, concat_axis=0, tiled=True),
        lax.all_to_all(value_rows, "tp", split_axis=1, concat_axis=0, tiled=True),
        lax.all_to_all(out_grad, "tp", split_axis=1, concat_axis=0, tiled=True),
    )
    length = query_here.shape[0]
    kv_heads = key_here.shape[1] // HD
    query_heads = query_here.reshape(length, kv_heads, per_kv, HD)
    grad_heads = grad_here.reshape(length, kv_heads, per_kv, HD)
    seq_count = lax.axis_size("seq")
    position = lax.axis_index("seq")
    doc_ends = jnp.cumsum(doc_lengths)
    first_query = position * length
    query_pos, query_seg = placed(first_query, length, doc_ends)
    first_seg = segment_of(first_query, doc_ends)
    reach = min((length - 1 + LONG - 1) // length, seq_count - 1)

    key_value = jnp.stack((key_here, value_here))
    gathered = [key_value] + [shifted(key_value, "seq", d) for d in range(1, reach + 1)]

    def block_mask(d):
        first_key = first_query - d * length
        key_pos, key_seg = placed(first_key, length, doc_ends)
        visible = allowed(query_pos, query_seg, key_pos, key_seg)
        if d == 0:
            live = jnp.bool_(True)
        else:
            last_key = first_key + length - 1
            live = (last_key >= 0) & (segment_of(last_key, doc_ends) == first_seg)
        return visible, live

    softmax_state = (
        jnp.full((length, kv_heads, per_kv), -1e30, jnp.float32),
        jnp.zeros((length, kv_heads, per_kv), jnp.float32),
        jnp.zeros((length, kv_heads, per_kv, HD), jnp.float32),
    )
    for d in range(reach + 1):
        visible, live = block_mask(d)
        key_block = gathered[d][0].reshape(length, kv_heads, HD)
        value_block = gathered[d][1].reshape(length, kv_heads, HD)
        softmax_state = lax.cond(
            live,
            lambda carried, kb=key_block, vb=value_block, vis=visible: absorb(
                carried, query_heads, kb, vb, vis, scaling
            ),
            lambda carried: carried,
            softmax_state,
        )
    running, denominator, accumulated = softmax_state
    out_heads = (accumulated / denominator[..., None]).astype(jnp.bfloat16)
    log_total = running + jnp.log(denominator)
    row_dot = jnp.sum(grad_heads.astype(jnp.float32) * out_heads.astype(jnp.float32), axis=-1)

    query_acc = jnp.zeros((length, kv_heads, per_kv, HD), jnp.float32)
    grad_sums = None
    for d in range(reach + 1):
        visible, live = block_mask(d)
        key_block = gathered[d][0].reshape(length, kv_heads, HD)
        value_block = gathered[d][1].reshape(length, kv_heads, HD)

        def compute(unused, kb=key_block, vb=value_block, vis=visible):
            query_part, key_part, value_part = contrib(
                query_heads, grad_heads, log_total, row_dot, kb, vb, vis, scaling
            )
            return (
                query_part,
                jnp.stack((key_part.reshape(length, -1), value_part.reshape(length, -1))),
            )

        def nothing(unused):
            return (
                jnp.zeros((length, kv_heads, per_kv, HD), jnp.float32),
                jnp.zeros((2, length, kv_heads * HD), jnp.float32),
            )

        query_part, key_value_part = lax.cond(live, compute, nothing, 0)
        query_acc = query_acc + query_part
        if d > 0:
            key_value_part = shifted(key_value_part, "seq", -d)
        grad_sums = key_value_part if grad_sums is None else grad_sums + key_value_part

    outputs = (
        lax.all_to_all(
            out_heads.reshape(length, -1), "tp", split_axis=0, concat_axis=1, tiled=True
        ),
        lax.all_to_all(
            query_acc.astype(jnp.bfloat16).reshape(length, -1),
            "tp",
            split_axis=0,
            concat_axis=1,
            tiled=True,
        ),
        lax.all_to_all(
            grad_sums[0].astype(jnp.bfloat16), "tp", split_axis=0, concat_axis=1, tiled=True
        ),
        lax.all_to_all(
            grad_sums[1].astype(jnp.bfloat16), "tp", split_axis=0, concat_axis=1, tiled=True
        ),
    )
    return (outputs[0], outputs[1], outputs[2], outputs[3])


def solution(mesh):
    return jax.shard_map(
        per_device,
        mesh=mesh,
        in_specs=(
            P(("seq", "tp"), None),
            P(("seq", "tp"), None),
            P(("seq", "tp"), None),
            P(("seq", "tp"), None),
            P(),
        ),
        out_specs=(
            P(("seq", "tp"), None),
            P(("seq", "tp"), None),
            P(("seq", "tp"), None),
            P(("seq", "tp"), None),
        ),
        check_vma=False,
    )
```

```python
import functools

import jax
import jax.numpy as jnp
from jax import lax
from jax.experimental import pallas as pl
from jax.experimental.pallas import tpu as pltpu
from jax.sharding import PartitionSpec as P

HD = 128
QH = 20
KVH = 4
LONG = 4096

NT = (((1,), (1,)), ((), ()))
TN = (((0,), (0,)), ((), ()))


def shifted(value, axis, by):
    peers = lax.axis_size(axis)
    pairs = [(i, i + by) for i in range(peers) if 0 <= i + by < peers]
    return lax.ppermute(value, axis, pairs)


def segment_of(position, doc_ends):
    return jnp.sum((position >= doc_ends).astype(jnp.int32))


def segments(first_row, row_count, doc_ends):
    position = first_row + jnp.arange(row_count, dtype=jnp.int32)
    return jnp.sum((position[:, None] >= doc_ends[None, :]).astype(jnp.int32), axis=1)


def block_visible(qseg_ref, kseg_ref, diagonal):
    visible = qseg_ref[...] == kseg_ref[...]
    if diagonal:
        rows = lax.broadcasted_iota(jnp.int32, visible.shape, 0)
        cols = lax.broadcasted_iota(jnp.int32, visible.shape, 1)
        visible = visible & (cols <= rows)
    return visible


def forward_kernel(live_ref, q_ref, k_ref, v_ref, qseg_ref, kseg_ref, m_in, l_in, acc_in,
                   m_out, l_out, acc_out, *, diagonal, scaling):
    @pl.when(live_ref[0] != 0)
    def _():
        scores = lax.dot_general(q_ref[...], k_ref[...], NT, preferred_element_type=jnp.float32)
        scores = scores * scaling
        visible = block_visible(qseg_ref, kseg_ref, diagonal)
        scores = jnp.where(visible, scores, -1e30)
        running = m_in[0][:, :1]
        newest = jnp.maximum(running, jnp.max(scores, axis=1, keepdims=True))
        weight = jnp.where(visible, jnp.exp(scores - newest), 0.0)
        shrink = jnp.exp(running - newest)
        denominator = l_in[0][:, :1] * shrink + jnp.sum(weight, axis=1, keepdims=True)
        mixed = jnp.dot(weight.astype(jnp.bfloat16), v_ref[...], preferred_element_type=jnp.float32)
        acc_out[...] = acc_in[...] * shrink + mixed
        m_out[0] = jnp.broadcast_to(newest, m_out.shape[1:])
        l_out[0] = jnp.broadcast_to(denominator, l_out.shape[1:])

    @pl.when(live_ref[0] == 0)
    def _():
        acc_out[...] = acc_in[...]
        m_out[...] = m_in[...]
        l_out[...] = l_in[...]


def backward_kernel(live_ref, q_ref, g_ref, lse_ref, dot_ref, k_ref, v_ref, qseg_ref, kseg_ref,
                    dq_in, dq_out, dk_out, dv_out, *, diagonal, scaling):
    head = pl.program_id(0)

    @pl.when(head == 0)
    def _():
        dk_out[...] = jnp.zeros_like(dk_out)
        dv_out[...] = jnp.zeros_like(dv_out)

    @pl.when(live_ref[0] != 0)
    def _():
        q = q_ref[...]
        g = g_ref[...]
        k = k_ref[...]
        scores = lax.dot_general(q, k, NT, preferred_element_type=jnp.float32) * scaling
        visible = block_visible(qseg_ref, kseg_ref, diagonal)
        scores = jnp.where(visible, scores, -1e30)
        probability = jnp.where(visible, jnp.exp(scores - lse_ref[0][:, :1]), 0.0)
        dv_out[...] += lax.dot_general(
            probability.astype(jnp.bfloat16), g, TN, preferred_element_type=jnp.float32
        )
        grad_prob = lax.dot_general(g, v_ref[...], NT, preferred_element_type=jnp.float32)
        grad_score = (probability * (grad_prob - dot_ref[0][:, :1])).astype(jnp.bfloat16)
        dq_out[...] = dq_in[...] + jnp.dot(grad_score, k, preferred_element_type=jnp.float32) * scaling
        dk_out[...] += lax.dot_general(grad_score, q, TN, preferred_element_type=jnp.float32) * scaling

    @pl.when(live_ref[0] == 0)
    def _():
        dq_out[...] = dq_in[...]


def forward_block(live, query, key, value, qseg, kseg, state, diagonal, scaling):
    length, width = query.shape
    heads = width // HD
    m, l, acc = state
    row_block = pl.BlockSpec((length, HD), lambda h, lv: (0, h))
    whole = pl.BlockSpec((length, HD), lambda h, lv: (0, 0))
    stat = pl.BlockSpec((1, length, HD), lambda h, lv: (h, 0, 0))
    grid_spec = pltpu.PrefetchScalarGridSpec(
        num_scalar_prefetch=1,
        grid=(heads,),
        in_specs=[
            row_block,
            whole,
            whole,
            pl.BlockSpec((length, 1), lambda h, lv: (0, 0)),
            pl.BlockSpec((1, length), lambda h, lv: (0, 0)),
            stat,
            stat,
            row_block,
        ],
        out_specs=[stat, stat, row_block],
    )
    return pl.pallas_call(
        functools.partial(forward_kernel, diagonal=diagonal, scaling=scaling),
        out_shape=(
            jax.ShapeDtypeStruct(m.shape, jnp.float32),
            jax.ShapeDtypeStruct(l.shape, jnp.float32),
            jax.ShapeDtypeStruct(acc.shape, jnp.float32),
        ),
        grid_spec=grid_spec,
        input_output_aliases={6: 0, 7: 1, 8: 2},
        cost_estimate=pl.CostEstimate(
            flops=4 * length * length * width,
            transcendentals=length * length * heads,
            bytes_accessed=40 * length * width,
        ),
        compiler_params=pltpu.CompilerParams(dimension_semantics=("arbitrary",)),
    )(live, query, key, value, qseg, kseg, m, l, acc)


def backward_block(live, query, grad, lse, rdot, key, value, qseg, kseg, dq, diagonal, scaling):
    length, width = query.shape
    heads = width // HD
    row_block = pl.BlockSpec((length, HD), lambda h, lv: (0, h))
    whole = pl.BlockSpec((length, HD), lambda h, lv: (0, 0))
    stat = pl.BlockSpec((1, length, HD), lambda h, lv: (h, 0, 0))
    grid_spec = pltpu.PrefetchScalarGridSpec(
        num_scalar_prefetch=1,
        grid=(heads,),
        in_specs=[
            row_block,
            row_block,
            stat,
            stat,
            whole,
            whole,
            pl.BlockSpec((length, 1), lambda h, lv: (0, 0)),
            pl.BlockSpec((1, length), lambda h, lv: (0, 0)),
            row_block,
        ],
        out_specs=[row_block, whole, whole],
    )
    return pl.pallas_call(
        functools.partial(backward_kernel, diagonal=diagonal, scaling=scaling),
        out_shape=(
            jax.ShapeDtypeStruct(dq.shape, jnp.float32),
            jax.ShapeDtypeStruct((length, HD), jnp.float32),
            jax.ShapeDtypeStruct((length, HD), jnp.float32),
        ),
        grid_spec=grid_spec,
        input_output_aliases={9: 0},
        cost_estimate=pl.CostEstimate(
            flops=10 * length * length * width,
            transcendentals=length * length * heads,
            bytes_accessed=40 * length * width,
        ),
        compiler_params=pltpu.CompilerParams(dimension_semantics=("arbitrary",)),
    )(live, query, grad, lse, rdot, key, value, qseg, kseg, dq)


def per_device(query_rows, key_rows, value_rows, out_grad, doc_lengths):
    per_kv = QH // KVH
    scaling = HD ** (-0.5)
    query_here, key_here, value_here, grad_here = (
        lax.all_to_all(query_rows, "tp", split_axis=1, concat_axis=0, tiled=True),
        lax.all_to_all(key_rows, "tp", split_axis=1, concat_axis=0, tiled=True),
        lax.all_to_all(value_rows, "tp", split_axis=1, concat_axis=0, tiled=True),
        lax.all_to_all(out_grad, "tp", split_axis=1, concat_axis=0, tiled=True),
    )
    length = query_here.shape[0]
    heads = query_here.shape[1] // HD
    seq_count = lax.axis_size("seq")
    position = lax.axis_index("seq")
    doc_ends = jnp.cumsum(doc_lengths)
    first_query = position * length
    qseg = segments(first_query, length, doc_ends).reshape(length, 1)
    first_seg = segment_of(first_query, doc_ends)
    reach = min((length - 1 + LONG - 1) // length, seq_count - 1)

    key_value = jnp.stack((key_here, value_here))
    gathered = [key_value] + [shifted(key_value, "seq", d) for d in range(1, reach + 1)]

    lives = []
    ksegs = []
    for d in range(reach + 1):
        first_key = first_query - d * length
        ksegs.append(segments(first_key, length, doc_ends).reshape(1, length))
        if d == 0:
            live = jnp.int32(1)
        else:
            last_key = first_key + length - 1
            live = ((last_key >= 0) & (segment_of(last_key, doc_ends) == first_seg)).astype(jnp.int32)
        lives.append(live.reshape(1))

    state = (
        jnp.full((heads, length, HD), -1e30, jnp.float32),
        jnp.zeros((heads, length, HD), jnp.float32),
        jnp.zeros((length, heads * HD), jnp.float32),
    )
    for d in range(reach + 1):
        state = forward_block(
            lives[d], query_here, gathered[d][0], gathered[d][1], qseg, ksegs[d], state,
            d == 0, scaling,
        )
    m, l, acc = state
    denominator = l[:, :, 0].T
    out_flat = (acc.reshape(length, heads, HD) / denominator[:, :, None]).astype(jnp.bfloat16)
    lse = m + jnp.log(l)
    rdot = jnp.sum(
        grad_here.reshape(length, heads, HD).astype(jnp.float32) * out_flat.astype(jnp.float32),
        axis=-1,
    )
    rdot = jnp.broadcast_to(rdot.T[:, :, None], (heads, length, HD))
    out_flat = out_flat.reshape(length, heads * HD)

    dq = jnp.zeros((length, heads * HD), jnp.float32)
    grad_sums = None
    for d in range(reach, -1, -1):
        dq, dk, dv = backward_block(
            lives[d], query_here, grad_here, lse, rdot, gathered[d][0], gathered[d][1],
            qseg, ksegs[d], dq, d == 0, scaling,
        )
        part = jnp.stack((dk, dv))
        if d > 0:
            part = shifted(part, "seq", -d)
        grad_sums = part if grad_sums is None else grad_sums + part

    outputs = (
        lax.all_to_all(out_flat, "tp", split_axis=0, concat_axis=1, tiled=True),
        lax.all_to_all(dq.astype(jnp.bfloat16), "tp", split_axis=0, concat_axis=1, tiled=True),
        lax.all_to_all(
            grad_sums[0].astype(jnp.bfloat16), "tp", split_axis=0, concat_axis=1, tiled=True
        ),
        lax.all_to_all(
            grad_sums[1].astype(jnp.bfloat16), "tp", split_axis=0, concat_axis=1, tiled=True
        ),
    )
    return outputs


def solution(mesh):
    return jax.shard_map(
        per_device,
        mesh=mesh,
        in_specs=(
            P(("seq", "tp"), None),
            P(("seq", "tp"), None),
            P(("seq", "tp"), None),
            P(("seq", "tp"), None),
            P(),
        ),
        out_specs=(
            P(("seq", "tp"), None),
            P(("seq", "tp"), None),
            P(("seq", "tp"), None),
            P(("seq", "tp"), None),
        ),
        check_vma=False,
    )
```

```python
import jax
import jax.numpy as jnp
from jax import lax
from jax.sharding import PartitionSpec as P

HD = 128
QH = 20
KVH = 4
LONG = 4096


def shifted(value, axis, by):
    peers = lax.axis_size(axis)
    pairs = [(i, i + by) for i in range(peers) if 0 <= i + by < peers]
    return lax.ppermute(value, axis, pairs)


def placed(first_row, row_count, doc_ends):
    position = first_row + jnp.arange(row_count, dtype=jnp.int32)
    segment = jnp.sum((position[:, None] >= doc_ends[None, :]).astype(jnp.int32), axis=1)
    return (position, segment)


def allowed(query_pos, query_seg, key_pos, key_seg):
    return (
        (key_pos[None, :] <= query_pos[:, None])
        & (key_pos[None, :] >= 0)
        & (key_seg[None, :] == query_seg[:, None])
    )


def absorb(softmax_state, query_heads, key_block, value_block, visible, scaling):
    running, denominator, accumulated = softmax_state
    scores = (
        jnp.einsum("bkgd,tkd->bkgt", query_heads, key_block, preferred_element_type=jnp.float32)
        * scaling
    )
    spread = visible[:, None, None, :]
    scores = jnp.where(spread, scores, -1e30)
    newest = jnp.maximum(running, jnp.max(scores, axis=-1))
    weight = jnp.where(spread, jnp.exp(scores - newest[..., None]), 0.0)
    shrink = jnp.exp(running - newest)
    denominator = denominator * shrink + jnp.sum(weight, axis=-1)
    accumulated = accumulated * shrink[..., None] + jnp.einsum(
        "bkgt,tkd->bkgd",
        weight.astype(jnp.bfloat16),
        value_block,
        preferred_element_type=jnp.float32,
    )
    return (newest, denominator, accumulated)


def contrib(query_heads, grad_heads, log_total, row_dot, key_block, value_block, visible, scaling):
    scores = (
        jnp.einsum("bkgd,tkd->bkgt", query_heads, key_block, preferred_element_type=jnp.float32)
        * scaling
    )
    spread = visible[:, None, None, :]
    scores = jnp.where(spread, scores, -1e30)
    probability = jnp.where(spread, jnp.exp(scores - log_total[..., None]), 0.0)
    value_part = jnp.einsum(
        "bkgt,bkgd->tkd",
        probability.astype(jnp.bfloat16),
        grad_heads,
        preferred_element_type=jnp.float32,
    )
    grad_prob = jnp.einsum(
        "bkgd,tkd->bkgt", grad_heads, value_block, preferred_element_type=jnp.float32
    )
    grad_score = (probability * (grad_prob - row_dot[..., None])).astype(jnp.bfloat16)
    query_part = (
        jnp.einsum("bkgt,tkd->bkgd", grad_score, key_block, preferred_element_type=jnp.float32)
        * scaling
    )
    key_part = (
        jnp.einsum("bkgt,bkgd->tkd", grad_score, query_heads, preferred_element_type=jnp.float32)
        * scaling
    )
    return (query_part, key_part, value_part)


def to_heads(arrays, groups):
    rows = arrays[0].shape[0]
    widths = [a.shape[1] // groups for a in arrays]
    joined = jnp.concatenate([a.reshape(rows, groups, -1) for a in arrays], axis=2)
    moved = lax.all_to_all(joined, "tp", split_axis=1, concat_axis=0, tiled=True)
    moved = moved.reshape(rows * groups, -1)
    pieces = []
    start = 0
    for w in widths:
        pieces.append(moved[:, start:start + w])
        start += w
    return pieces


def from_heads(arrays, groups):
    rows = arrays[0].shape[0] // groups
    widths = [a.shape[1] for a in arrays]
    joined = jnp.concatenate(arrays, axis=1).reshape(groups, rows, 1, -1)
    moved = lax.all_to_all(joined, "tp", split_axis=0, concat_axis=2, tiled=True)
    moved = moved.reshape(rows, groups, -1)
    pieces = []
    start = 0
    for w in widths:
        pieces.append(moved[:, :, start:start + w].reshape(rows, groups * w))
        start += w
    return pieces


def per_device(query_rows, key_rows, value_rows, out_grad, doc_lengths):
    per_kv = QH // KVH
    scaling = HD ** (-0.5)
    groups = lax.axis_size("tp")
    query_here, key_here, value_here = to_heads([query_rows, key_rows, value_rows], groups)
    (grad_here,) = to_heads([out_grad], groups)
    length = query_here.shape[0]
    kv_heads = key_here.shape[1] // HD
    query_heads = query_here.reshape(length, kv_heads, per_kv, HD)
    grad_heads = grad_here.reshape(length, kv_heads, per_kv, HD)
    seq_count = lax.axis_size("seq")
    position = lax.axis_index("seq")
    doc_ends = jnp.cumsum(doc_lengths)
    first_query = position * length
    query_pos, query_seg = placed(first_query, length, doc_ends)
    reach = min((length - 1 + LONG - 1) // length, seq_count - 1)

    key_value = jnp.stack((key_here, value_here))
    gathered = [key_value] + [shifted(key_value, "seq", d) for d in range(1, reach + 1)]

    def block_mask(d):
        key_pos, key_seg = placed(first_query - d * length, length, doc_ends)
        return allowed(query_pos, query_seg, key_pos, key_seg)

    softmax_state = (
        jnp.full((length, kv_heads, per_kv), -1e30, jnp.float32),
        jnp.zeros((length, kv_heads, per_kv), jnp.float32),
        jnp.zeros((length, kv_heads, per_kv, HD), jnp.float32),
    )
    for d in range(reach + 1):
        softmax_state, block = lax.optimization_barrier((softmax_state, gathered[d]))
        key_block = block[0].reshape(length, kv_heads, HD)
        value_block = block[1].reshape(length, kv_heads, HD)
        softmax_state = absorb(
            softmax_state, query_heads, key_block, value_block, block_mask(d), scaling
        )
    running, denominator, accumulated = softmax_state
    out_heads = (accumulated / denominator[..., None]).astype(jnp.bfloat16)
    log_total = running + jnp.log(denominator)
    row_dot = jnp.sum(grad_heads.astype(jnp.float32) * out_heads.astype(jnp.float32), axis=-1)

    query_acc = jnp.zeros((length, kv_heads, per_kv, HD), jnp.float32)
    sent = {}
    for d in range(reach, -1, -1):
        arrived = sent.pop(d + 2, None)
        if arrived is None:
            query_acc, block = lax.optimization_barrier((query_acc, gathered[d]))
        else:
            query_acc, block, arrived = lax.optimization_barrier((query_acc, gathered[d], arrived))
            sent[("in", d + 2)] = arrived
        key_block = block[0].reshape(length, kv_heads, HD)
        value_block = block[1].reshape(length, kv_heads, HD)
        query_part, key_part, value_part = contrib(
            query_heads, grad_heads, log_total, row_dot, key_block, value_block,
            block_mask(d), scaling,
        )
        query_acc = query_acc + query_part
        part = jnp.stack((key_part.reshape(length, -1), value_part.reshape(length, -1)))
        if d > 0:
            sent[d] = shifted(part.astype(jnp.bfloat16), "seq", -d)
        else:
            own = part
    grad_sums = own
    for received in sent.values():
        grad_sums = grad_sums + received.astype(jnp.float32)

    return tuple(
        from_heads(
            [
                out_heads.reshape(length, -1),
                query_acc.astype(jnp.bfloat16).reshape(length, -1),
                grad_sums[0].astype(jnp.bfloat16),
                grad_sums[1].astype(jnp.bfloat16),
            ],
            groups,
        )
    )


def solution(mesh):
    return jax.shard_map(
        per_device,
        mesh=mesh,
        in_specs=(
            P(("seq", "tp"), None),
            P(("seq", "tp"), None),
            P(("seq", "tp"), None),
            P(("seq", "tp"), None),
            P(),
        ),
        out_specs=(
            P(("seq", "tp"), None),
            P(("seq", "tp"), None),
            P(("seq", "tp"), None),
            P(("seq", "tp"), None),
        ),
        check_vma=False,
    )
```

```python
import jax
import jax.numpy as jnp
from jax import lax
from jax.sharding import PartitionSpec as P

HD = 128
QH = 20
KVH = 4
LONG = 4096


def shifted(value, axis, by):
    peers = lax.axis_size(axis)
    pairs = [(i, i + by) for i in range(peers) if 0 <= i + by < peers]
    return lax.ppermute(value, axis, pairs)


def placed(first_row, row_count, doc_ends):
    position = first_row + jnp.arange(row_count, dtype=jnp.int32)
    segment = jnp.sum((position[:, None] >= doc_ends[None, :]).astype(jnp.int32), axis=1)
    return (position, segment)


def allowed(query_pos, query_seg, key_pos, key_seg):
    return (
        (key_pos[None, :] <= query_pos[:, None])
        & (key_pos[None, :] >= 0)
        & (key_seg[None, :] == query_seg[:, None])
    )


def absorb(softmax_state, query_heads, key_block, value_block, visible, scaling):
    running, denominator, accumulated = softmax_state
    scores = (
        jnp.einsum("bkgd,tkd->bkgt", query_heads, key_block, preferred_element_type=jnp.float32)
        * scaling
    )
    spread = visible[:, None, None, :]
    scores = jnp.where(spread, scores, -1e30)
    newest = jnp.maximum(running, jnp.max(scores, axis=-1))
    weight = jnp.where(spread, jnp.exp(scores - newest[..., None]), 0.0)
    shrink = jnp.exp(running - newest)
    denominator = denominator * shrink + jnp.sum(weight, axis=-1)
    accumulated = accumulated * shrink[..., None] + jnp.einsum(
        "bkgt,tkd->bkgd",
        weight.astype(jnp.bfloat16),
        value_block,
        preferred_element_type=jnp.float32,
    )
    return (newest, denominator, accumulated)


def contrib(query_heads, grad_heads, log_total, row_dot, key_block, value_block, visible, scaling):
    scores = (
        jnp.einsum("bkgd,tkd->bkgt", query_heads, key_block, preferred_element_type=jnp.float32)
        * scaling
    )
    spread = visible[:, None, None, :]
    scores = jnp.where(spread, scores, -1e30)
    probability = jnp.where(spread, jnp.exp(scores - log_total[..., None]), 0.0)
    value_part = jnp.einsum(
        "bkgt,bkgd->tkd",
        probability.astype(jnp.bfloat16),
        grad_heads,
        preferred_element_type=jnp.float32,
    )
    grad_prob = jnp.einsum(
        "bkgd,tkd->bkgt", grad_heads, value_block, preferred_element_type=jnp.float32
    )
    grad_score = (probability * (grad_prob - row_dot[..., None])).astype(jnp.bfloat16)
    query_part = (
        jnp.einsum("bkgt,tkd->bkgd", grad_score, key_block, preferred_element_type=jnp.float32)
        * scaling
    )
    key_part = (
        jnp.einsum("bkgt,bkgd->tkd", grad_score, query_heads, preferred_element_type=jnp.float32)
        * scaling
    )
    return (query_part, key_part, value_part)


def to_heads(arrays, groups):
    rows = arrays[0].shape[0]
    widths = [a.shape[1] // groups for a in arrays]
    joined = jnp.concatenate([a.reshape(rows, groups, -1) for a in arrays], axis=2)
    moved = lax.all_to_all(joined, "tp", split_axis=1, concat_axis=0, tiled=True)
    moved = moved.reshape(rows * groups, -1)
    pieces = []
    start = 0
    for w in widths:
        pieces.append(moved[:, start:start + w])
        start += w
    return pieces


def from_heads(arrays, groups):
    rows = arrays[0].shape[0] // groups
    widths = [a.shape[1] for a in arrays]
    joined = jnp.concatenate(arrays, axis=1).reshape(groups, rows, 1, -1)
    moved = lax.all_to_all(joined, "tp", split_axis=0, concat_axis=2, tiled=True)
    moved = moved.reshape(rows, groups, -1)
    pieces = []
    start = 0
    for w in widths:
        pieces.append(moved[:, :, start:start + w].reshape(rows, groups * w))
        start += w
    return pieces


def per_device(query_rows, key_rows, value_rows, out_grad, doc_lengths):
    per_kv = QH // KVH
    scaling = HD ** (-0.5)
    groups = lax.axis_size("tp")
    key_here, value_here = to_heads([key_rows, value_rows], groups)
    (query_here,) = to_heads([query_rows], groups)
    (grad_here,) = to_heads([out_grad], groups)
    length = query_here.shape[0]
    kv_heads = key_here.shape[1] // HD
    query_heads = query_here.reshape(length, kv_heads, per_kv, HD)
    grad_heads = grad_here.reshape(length, kv_heads, per_kv, HD)
    seq_count = lax.axis_size("seq")
    position = lax.axis_index("seq")
    doc_ends = jnp.cumsum(doc_lengths)
    first_query = position * length
    query_pos, query_seg = placed(first_query, length, doc_ends)
    reach = min((length - 1 + LONG - 1) // length, seq_count - 1)

    key_value = jnp.stack((key_here, value_here))
    gathered = [key_value] + [shifted(key_value, "seq", d) for d in range(1, reach + 1)]

    def block_mask(d):
        key_pos, key_seg = placed(first_query - d * length, length, doc_ends)
        return allowed(query_pos, query_seg, key_pos, key_seg)

    softmax_state = (
        jnp.full((length, kv_heads, per_kv), -1e30, jnp.float32),
        jnp.zeros((length, kv_heads, per_kv), jnp.float32),
        jnp.zeros((length, kv_heads, per_kv, HD), jnp.float32),
    )
    for d in range(reach + 1):
        softmax_state, block = lax.optimization_barrier((softmax_state, gathered[d]))
        key_block = block[0].reshape(length, kv_heads, HD)
        value_block = block[1].reshape(length, kv_heads, HD)
        softmax_state = absorb(
            softmax_state, query_heads, key_block, value_block, block_mask(d), scaling
        )
    running, denominator, accumulated = softmax_state
    out_heads = (accumulated / denominator[..., None]).astype(jnp.bfloat16)
    log_total = running + jnp.log(denominator)
    row_dot = jnp.sum(grad_heads.astype(jnp.float32) * out_heads.astype(jnp.float32), axis=-1)
    (attended,) = from_heads([out_heads.reshape(length, -1)], groups)

    query_acc = jnp.zeros((length, kv_heads, per_kv, HD), jnp.float32)
    sent = {}
    for d in range(reach, -1, -1):
        arrived = sent.pop(d + 2, None)
        if arrived is None:
            query_acc, block = lax.optimization_barrier((query_acc, gathered[d]))
        else:
            query_acc, block, arrived = lax.optimization_barrier((query_acc, gathered[d], arrived))
            sent[("in", d + 2)] = arrived
        key_block = block[0].reshape(length, kv_heads, HD)
        value_block = block[1].reshape(length, kv_heads, HD)
        query_part, key_part, value_part = contrib(
            query_heads, grad_heads, log_total, row_dot, key_block, value_block,
            block_mask(d), scaling,
        )
        query_acc = query_acc + query_part
        part = jnp.stack((key_part.reshape(length, -1), value_part.reshape(length, -1)))
        if d > 0:
            sent[d] = shifted(part.astype(jnp.bfloat16), "seq", -d)
        else:
            own = part
    grad_sums = own
    for received in sent.values():
        grad_sums = grad_sums + received.astype(jnp.float32)

    return (attended,) + tuple(
        from_heads(
            [
                query_acc.astype(jnp.bfloat16).reshape(length, -1),
                grad_sums[0].astype(jnp.bfloat16),
                grad_sums[1].astype(jnp.bfloat16),
            ],
            groups,
        )
    )


def solution(mesh):
    return jax.shard_map(
        per_device,
        mesh=mesh,
        in_specs=(
            P(("seq", "tp"), None),
            P(("seq", "tp"), None),
            P(("seq", "tp"), None),
            P(("seq", "tp"), None),
            P(),
        ),
        out_specs=(
            P(("seq", "tp"), None),
            P(("seq", "tp"), None),
            P(("seq", "tp"), None),
            P(("seq", "tp"), None),
        ),
        check_vma=False,
    )
```

```python
import jax
import jax.numpy as jnp
from jax import lax
from jax.sharding import PartitionSpec as P

HD = 128
QH = 20
KVH = 4
LONG = 4096


def shifted(value, axis, by):
    peers = lax.axis_size(axis)
    pairs = [(i, i + by) for i in range(peers) if 0 <= i + by < peers]
    return lax.ppermute(value, axis, pairs)


def placed(first_row, row_count, doc_ends):
    position = first_row + jnp.arange(row_count, dtype=jnp.int32)
    segment = jnp.sum((position[:, None] >= doc_ends[None, :]).astype(jnp.int32), axis=1)
    return (position, segment)


def allowed(query_pos, query_seg, key_pos, key_seg):
    return (
        (key_pos[None, :] <= query_pos[:, None])
        & (key_pos[None, :] >= 0)
        & (key_seg[None, :] == query_seg[:, None])
    )


def absorb(softmax_state, query_heads, key_block, value_block, visible, scaling):
    running, denominator, accumulated = softmax_state
    scores = (
        jnp.einsum("bkgd,tkd->bkgt", query_heads, key_block, preferred_element_type=jnp.float32)
        * scaling
    )
    spread = visible[:, None, None, :]
    scores = jnp.where(spread, scores, -1e30)
    newest = jnp.maximum(running, jnp.max(scores, axis=-1))
    weight = jnp.where(spread, jnp.exp(scores - newest[..., None]), 0.0)
    shrink = jnp.exp(running - newest)
    denominator = denominator * shrink + jnp.sum(weight, axis=-1)
    accumulated = accumulated * shrink[..., None] + jnp.einsum(
        "bkgt,tkd->bkgd",
        weight.astype(jnp.bfloat16),
        value_block,
        preferred_element_type=jnp.float32,
    )
    return (newest, denominator, accumulated)


def contrib(query_heads, grad_heads, log_total, row_dot, key_block, value_block, visible, scaling):
    scores = (
        jnp.einsum("bkgd,tkd->bkgt", query_heads, key_block, preferred_element_type=jnp.float32)
        * scaling
    )
    spread = visible[:, None, None, :]
    scores = jnp.where(spread, scores, -1e30)
    probability = jnp.where(spread, jnp.exp(scores - log_total[..., None]), 0.0)
    value_part = jnp.einsum(
        "bkgt,bkgd->tkd",
        probability.astype(jnp.bfloat16),
        grad_heads,
        preferred_element_type=jnp.float32,
    )
    grad_prob = jnp.einsum(
        "bkgd,tkd->bkgt", grad_heads, value_block, preferred_element_type=jnp.float32
    )
    grad_score = (probability * (grad_prob - row_dot[..., None])).astype(jnp.bfloat16)
    query_part = (
        jnp.einsum("bkgt,tkd->bkgd", grad_score, key_block, preferred_element_type=jnp.float32)
        * scaling
    )
    key_part = (
        jnp.einsum("bkgt,bkgd->tkd", grad_score, query_heads, preferred_element_type=jnp.float32)
        * scaling
    )
    return (query_part, key_part, value_part)


def to_heads(arrays, groups):
    rows = arrays[0].shape[0]
    widths = [a.shape[1] // groups for a in arrays]
    joined = jnp.concatenate([a.reshape(rows, groups, -1) for a in arrays], axis=2)
    moved = lax.all_to_all(joined, "tp", split_axis=1, concat_axis=0, tiled=True)
    moved = moved.reshape(rows * groups, -1)
    pieces = []
    start = 0
    for w in widths:
        pieces.append(moved[:, start:start + w])
        start += w
    return pieces


def from_heads(arrays, groups):
    rows = arrays[0].shape[0] // groups
    widths = [a.shape[1] for a in arrays]
    joined = jnp.concatenate(arrays, axis=1).reshape(groups, rows, 1, -1)
    moved = lax.all_to_all(joined, "tp", split_axis=0, concat_axis=2, tiled=True)
    moved = moved.reshape(rows, groups, -1)
    pieces = []
    start = 0
    for w in widths:
        pieces.append(moved[:, :, start:start + w].reshape(rows, groups * w))
        start += w
    return pieces


def per_device(query_rows, key_rows, value_rows, out_grad, doc_lengths):
    per_kv = QH // KVH
    scaling = HD ** (-0.5)
    groups = lax.axis_size("tp")
    query_here, key_here, value_here = to_heads([query_rows, key_rows, value_rows], groups)
    (grad_here,) = to_heads([out_grad], groups)
    length = query_here.shape[0]
    kv_heads = key_here.shape[1] // HD
    query_heads = query_here.reshape(length, kv_heads, per_kv, HD)
    grad_heads = grad_here.reshape(length, kv_heads, per_kv, HD)
    seq_count = lax.axis_size("seq")
    position = lax.axis_index("seq")
    doc_ends = jnp.cumsum(doc_lengths)
    first_query = position * length
    query_pos, query_seg = placed(first_query, length, doc_ends)
    reach = min((length - 1 + LONG - 1) // length, seq_count - 1)

    key_value = jnp.stack((key_here, value_here))
    gathered = [key_value]
    while len(gathered) < reach + 1:
        step = len(gathered)
        take = min(step, reach + 1 - step)
        arrived = shifted(jnp.stack(gathered[:take]), "seq", step)
        gathered += [arrived[i] for i in range(take)]

    def block_mask(d):
        key_pos, key_seg = placed(first_query - d * length, length, doc_ends)
        return allowed(query_pos, query_seg, key_pos, key_seg)

    softmax_state = (
        jnp.full((length, kv_heads, per_kv), -1e30, jnp.float32),
        jnp.zeros((length, kv_heads, per_kv), jnp.float32),
        jnp.zeros((length, kv_heads, per_kv, HD), jnp.float32),
    )
    for d in range(reach + 1):
        softmax_state, block = lax.optimization_barrier((softmax_state, gathered[d]))
        key_block = block[0].reshape(length, kv_heads, HD)
        value_block = block[1].reshape(length, kv_heads, HD)
        softmax_state = absorb(
            softmax_state, query_heads, key_block, value_block, block_mask(d), scaling
        )
    running, denominator, accumulated = softmax_state
    out_heads = (accumulated / denominator[..., None]).astype(jnp.bfloat16)
    log_total = running + jnp.log(denominator)
    row_dot = jnp.sum(grad_heads.astype(jnp.float32) * out_heads.astype(jnp.float32), axis=-1)

    query_acc = jnp.zeros((length, kv_heads, per_kv, HD), jnp.float32)
    sent = {}
    for d in range(reach, -1, -1):
        arrived = sent.pop(d + 3, None)
        if arrived is None:
            query_acc, block = lax.optimization_barrier((query_acc, gathered[d]))
        else:
            query_acc, block, arrived = lax.optimization_barrier((query_acc, gathered[d], arrived))
            sent[("in", d + 3)] = arrived
        key_block = block[0].reshape(length, kv_heads, HD)
        value_block = block[1].reshape(length, kv_heads, HD)
        query_part, key_part, value_part = contrib(
            query_heads, grad_heads, log_total, row_dot, key_block, value_block,
            block_mask(d), scaling,
        )
        query_acc = query_acc + query_part
        part = jnp.stack((key_part.reshape(length, -1), value_part.reshape(length, -1)))
        if d > 0:
            sent[d] = shifted(part.astype(jnp.bfloat16), "seq", -d)
        else:
            own = part
    grad_sums = own
    for received in sent.values():
        grad_sums = grad_sums + received.astype(jnp.float32)

    return tuple(
        from_heads(
            [
                out_heads.reshape(length, -1),
                query_acc.astype(jnp.bfloat16).reshape(length, -1),
                grad_sums[0].astype(jnp.bfloat16),
                grad_sums[1].astype(jnp.bfloat16),
            ],
            groups,
        )
    )


def solution(mesh):
    return jax.shard_map(
        per_device,
        mesh=mesh,
        in_specs=(
            P(("seq", "tp"), None),
            P(("seq", "tp"), None),
            P(("seq", "tp"), None),
            P(("seq", "tp"), None),
            P(),
        ),
        out_specs=(
            P(("seq", "tp"), None),
            P(("seq", "tp"), None),
            P(("seq", "tp"), None),
            P(("seq", "tp"), None),
        ),
        check_vma=False,
    )
```

```python
import jax
import jax.numpy as jnp
from jax import lax
from jax.sharding import PartitionSpec as P

HD = 128
QH = 20
KVH = 4
LONG = 4096


def shifted(value, axis, by):
    peers = lax.axis_size(axis)
    pairs = [(i, i + by) for i in range(peers) if 0 <= i + by < peers]
    return lax.ppermute(value, axis, pairs)


def placed(first_row, row_count, doc_ends):
    position = first_row + jnp.arange(row_count, dtype=jnp.int32)
    segment = jnp.sum((position[:, None] >= doc_ends[None, :]).astype(jnp.int32), axis=1)
    return (position, segment)


def allowed(query_pos, query_seg, key_pos, key_seg):
    return (
        (key_pos[None, :] <= query_pos[:, None])
        & (key_pos[None, :] >= 0)
        & (key_seg[None, :] == query_seg[:, None])
    )


def absorb(softmax_state, query_heads, key_block, value_block, visible, scaling):
    running, denominator, accumulated = softmax_state
    scores = (
        jnp.einsum("bkgd,tkd->bkgt", query_heads, key_block, preferred_element_type=jnp.float32)
        * scaling
    )
    spread = visible[:, None, None, :]
    scores = jnp.where(spread, scores, -1e30)
    newest = jnp.maximum(running, jnp.max(scores, axis=-1))
    weight = jnp.where(spread, jnp.exp(scores - newest[..., None]), 0.0)
    shrink = jnp.exp(running - newest)
    denominator = denominator * shrink + jnp.sum(weight, axis=-1)
    accumulated = accumulated * shrink[..., None] + jnp.einsum(
        "bkgt,tkd->bkgd",
        weight.astype(jnp.bfloat16),
        value_block,
        preferred_element_type=jnp.float32,
    )
    return (newest, denominator, accumulated)


def contrib(query_heads, grad_heads, log_total, row_dot, key_block, value_block, visible, scaling):
    scores = (
        jnp.einsum("bkgd,tkd->bkgt", query_heads, key_block, preferred_element_type=jnp.float32)
        * scaling
    )
    spread = visible[:, None, None, :]
    scores = jnp.where(spread, scores, -1e30)
    probability = jnp.where(spread, jnp.exp(scores - log_total[..., None]), 0.0)
    value_part = jnp.einsum(
        "bkgt,bkgd->tkd",
        probability.astype(jnp.bfloat16),
        grad_heads,
        preferred_element_type=jnp.float32,
    )
    grad_prob = jnp.einsum(
        "bkgd,tkd->bkgt", grad_heads, value_block, preferred_element_type=jnp.float32
    )
    grad_score = (probability * (grad_prob - row_dot[..., None])).astype(jnp.bfloat16)
    query_part = (
        jnp.einsum("bkgt,tkd->bkgd", grad_score, key_block, preferred_element_type=jnp.float32)
        * scaling
    )
    key_part = (
        jnp.einsum("bkgt,bkgd->tkd", grad_score, query_heads, preferred_element_type=jnp.float32)
        * scaling
    )
    return (query_part, key_part, value_part)


def to_heads(arrays, groups):
    rows = arrays[0].shape[0]
    widths = [a.shape[1] // groups for a in arrays]
    joined = jnp.concatenate([a.reshape(rows, groups, -1) for a in arrays], axis=2)
    moved = lax.all_to_all(joined, "tp", split_axis=1, concat_axis=0, tiled=True)
    moved = moved.reshape(rows * groups, -1)
    pieces = []
    start = 0
    for w in widths:
        pieces.append(moved[:, start:start + w])
        start += w
    return pieces


def from_heads(arrays, groups):
    rows = arrays[0].shape[0] // groups
    widths = [a.shape[1] for a in arrays]
    joined = jnp.concatenate(arrays, axis=1).reshape(groups, rows, 1, -1)
    moved = lax.all_to_all(joined, "tp", split_axis=0, concat_axis=2, tiled=True)
    moved = moved.reshape(rows, groups, -1)
    pieces = []
    start = 0
    for w in widths:
        pieces.append(moved[:, :, start:start + w].reshape(rows, groups * w))
        start += w
    return pieces


def per_device(query_rows, key_rows, value_rows, out_grad, doc_lengths):
    per_kv = QH // KVH
    scaling = HD ** (-0.5)
    groups = lax.axis_size("tp")
    query_here, key_here, value_here = to_heads([query_rows, key_rows, value_rows], groups)
    length = query_here.shape[0]
    kv_heads = key_here.shape[1] // HD
    query_heads = query_here.reshape(length, kv_heads, per_kv, HD)
    seq_count = lax.axis_size("seq")
    position = lax.axis_index("seq")
    doc_ends = jnp.cumsum(doc_lengths)
    first_query = position * length
    query_pos, query_seg = placed(first_query, length, doc_ends)
    reach = min((length - 1 + LONG - 1) // length, seq_count - 1)

    key_value = jnp.stack((key_here, value_here))
    gathered = {0: key_value, 1: shifted(key_value, "seq", 1)}
    depth = {0: 0, 1: 1}
    pair = jnp.stack((gathered[0], gathered[1]))
    for step in range(2, reach + 1, 2):
        if step + 1 <= reach:
            arrived = shifted(pair, "seq", step)
            gathered[step], gathered[step + 1] = arrived[0], arrived[1]
            depth[step] = depth[step + 1] = 2
        else:
            gathered[step] = shifted(key_value, "seq", step)
            depth[step] = 1
    order = sorted(range(reach + 1), key=lambda d: (depth[d], d))

    def block_mask(d):
        key_pos, key_seg = placed(first_query - d * length, length, doc_ends)
        return allowed(query_pos, query_seg, key_pos, key_seg)

    softmax_state = (
        jnp.full((length, kv_heads, per_kv), -1e30, jnp.float32),
        jnp.zeros((length, kv_heads, per_kv), jnp.float32),
        jnp.zeros((length, kv_heads, per_kv, HD), jnp.float32),
    )
    for d in order:
        softmax_state, block = lax.optimization_barrier((softmax_state, gathered[d]))
        key_block = block[0].reshape(length, kv_heads, HD)
        value_block = block[1].reshape(length, kv_heads, HD)
        softmax_state = absorb(
            softmax_state, query_heads, key_block, value_block, block_mask(d), scaling
        )
        if d == 0:
            out_grad, softmax_state = lax.optimization_barrier((out_grad, softmax_state))
            (grad_here,) = to_heads([out_grad], groups)
            grad_heads = grad_here.reshape(length, kv_heads, per_kv, HD)
    running, denominator, accumulated = softmax_state
    out_heads = (accumulated / denominator[..., None]).astype(jnp.bfloat16)
    log_total = running + jnp.log(denominator)
    row_dot = jnp.sum(grad_heads.astype(jnp.float32) * out_heads.astype(jnp.float32), axis=-1)

    query_acc = jnp.zeros((length, kv_heads, per_kv, HD), jnp.float32)
    sent = {}
    for d in range(reach, -1, -1):
        arrived = sent.pop(d + 3, None)
        if arrived is None:
            query_acc, block = lax.optimization_barrier((query_acc, gathered[d]))
        else:
            query_acc, block, arrived = lax.optimization_barrier((query_acc, gathered[d], arrived))
            sent[("in", d + 3)] = arrived
        key_block = block[0].reshape(length, kv_heads, HD)
        value_block = block[1].reshape(length, kv_heads, HD)
        query_part, key_part, value_part = contrib(
            query_heads, grad_heads, log_total, row_dot, key_block, value_block,
            block_mask(d), scaling,
        )
        query_acc = query_acc + query_part
        part = jnp.stack((key_part.reshape(length, -1), value_part.reshape(length, -1)))
        if d > 0:
            sent[d] = shifted(part.astype(jnp.bfloat16), "seq", -d)
        else:
            own = part
    grad_sums = own
    for received in sent.values():
        grad_sums = grad_sums + received.astype(jnp.float32)

    return tuple(
        from_heads(
            [
                out_heads.reshape(length, -1),
                query_acc.astype(jnp.bfloat16).reshape(length, -1),
                grad_sums[0].astype(jnp.bfloat16),
                grad_sums[1].astype(jnp.bfloat16),
            ],
            groups,
        )
    )


def solution(mesh):
    return jax.shard_map(
        per_device,
        mesh=mesh,
        in_specs=(
            P(("seq", "tp"), None),
            P(("seq", "tp"), None),
            P(("seq", "tp"), None),
            P(("seq", "tp"), None),
            P(),
        ),
        out_specs=(
            P(("seq", "tp"), None),
            P(("seq", "tp"), None),
            P(("seq", "tp"), None),
            P(("seq", "tp"), None),
        ),
        check_vma=False,
    )
```

```python
import jax
import jax.numpy as jnp
from jax import lax
from jax.sharding import PartitionSpec as P

HD = 128
QH = 20
KVH = 4
LONG = 4096


def shifted(value, axis, by):
    peers = lax.axis_size(axis)
    pairs = [(i, i + by) for i in range(peers) if 0 <= i + by < peers]
    return lax.ppermute(value, axis, pairs)


def placed(first_row, row_count, doc_ends):
    position = first_row + jnp.arange(row_count, dtype=jnp.int32)
    segment = jnp.sum((position[:, None] >= doc_ends[None, :]).astype(jnp.int32), axis=1)
    return (position, segment)


def allowed(query_pos, query_seg, key_pos, key_seg):
    return (
        (key_pos[None, :] <= query_pos[:, None])
        & (key_pos[None, :] >= 0)
        & (key_seg[None, :] == query_seg[:, None])
    )


def absorb(softmax_state, query_heads, key_block, value_block, visible, scaling):
    running, denominator, accumulated = softmax_state
    scores = (
        jnp.einsum("bkgd,tkd->bkgt", query_heads, key_block, preferred_element_type=jnp.float32)
        * scaling
    )
    spread = visible[:, None, None, :]
    scores = jnp.where(spread, scores, -1e30)
    newest = jnp.maximum(running, jnp.max(scores, axis=-1))
    weight = jnp.where(spread, jnp.exp(scores - newest[..., None]), 0.0)
    shrink = jnp.exp(running - newest)
    denominator = denominator * shrink + jnp.sum(weight, axis=-1)
    accumulated = accumulated * shrink[..., None] + jnp.einsum(
        "bkgt,tkd->bkgd",
        weight.astype(jnp.bfloat16),
        value_block,
        preferred_element_type=jnp.float32,
    )
    return (newest, denominator, accumulated)


def contrib(query_heads, grad_heads, log_total, row_dot, key_block, value_block, visible, scaling):
    scores = (
        jnp.einsum("bkgd,tkd->bkgt", query_heads, key_block, preferred_element_type=jnp.float32)
        * scaling
    )
    spread = visible[:, None, None, :]
    scores = jnp.where(spread, scores, -1e30)
    probability = jnp.where(spread, jnp.exp(scores - log_total[..., None]), 0.0)
    value_part = jnp.einsum(
        "bkgt,bkgd->tkd",
        probability.astype(jnp.bfloat16),
        grad_heads,
        preferred_element_type=jnp.float32,
    )
    grad_prob = jnp.einsum(
        "bkgd,tkd->bkgt", grad_heads, value_block, preferred_element_type=jnp.float32
    )
    grad_score = (probability * (grad_prob - row_dot[..., None])).astype(jnp.bfloat16)
    query_part = (
        jnp.einsum("bkgt,tkd->bkgd", grad_score, key_block, preferred_element_type=jnp.float32)
        * scaling
    )
    key_part = (
        jnp.einsum("bkgt,bkgd->tkd", grad_score, query_heads, preferred_element_type=jnp.float32)
        * scaling
    )
    return (query_part, key_part, value_part)


def to_heads(arrays, groups):
    rows = arrays[0].shape[0]
    widths = [a.shape[1] // groups for a in arrays]
    joined = jnp.concatenate([a.reshape(rows, groups, -1) for a in arrays], axis=2)
    moved = lax.all_to_all(joined, "tp", split_axis=1, concat_axis=0, tiled=True)
    moved = moved.reshape(rows * groups, -1)
    pieces = []
    start = 0
    for w in widths:
        pieces.append(moved[:, start:start + w])
        start += w
    return pieces


def from_heads(arrays, groups):
    rows = arrays[0].shape[0] // groups
    widths = [a.shape[1] for a in arrays]
    joined = jnp.concatenate(arrays, axis=1).reshape(groups, rows, 1, -1)
    moved = lax.all_to_all(joined, "tp", split_axis=0, concat_axis=2, tiled=True)
    moved = moved.reshape(rows, groups, -1)
    pieces = []
    start = 0
    for w in widths:
        pieces.append(moved[:, :, start:start + w].reshape(rows, groups * w))
        start += w
    return pieces


def per_device(query_rows, key_rows, value_rows, out_grad, doc_lengths):
    per_kv = QH // KVH
    scaling = HD ** (-0.5)
    groups = lax.axis_size("tp")
    query_here, key_here, value_here = to_heads([query_rows, key_rows, value_rows], groups)
    (grad_here,) = to_heads([out_grad], groups)
    length = query_here.shape[0]
    kv_heads = key_here.shape[1] // HD
    query_heads = query_here.reshape(length, kv_heads, per_kv, HD)
    grad_heads = grad_here.reshape(length, kv_heads, per_kv, HD)
    seq_count = lax.axis_size("seq")
    position = lax.axis_index("seq")
    doc_ends = jnp.cumsum(doc_lengths)
    first_query = position * length
    query_pos, query_seg = placed(first_query, length, doc_ends)
    reach = min((length - 1 + LONG - 1) // length, seq_count - 1)

    key_value = jnp.stack((key_here, value_here))
    gathered = [key_value]
    steps = []
    while len(gathered) < reach + 1:
        step = len(gathered)
        take = min(step, reach + 1 - step)
        steps.append((step, take))
        arrived = shifted(jnp.stack(gathered[:take]), "seq", step)
        gathered += [arrived[i] for i in range(take)]

    def block_mask(d):
        key_pos, key_seg = placed(first_query - d * length, length, doc_ends)
        return allowed(query_pos, query_seg, key_pos, key_seg)

    softmax_state = (
        jnp.full((length, kv_heads, per_kv), -1e30, jnp.float32),
        jnp.zeros((length, kv_heads, per_kv), jnp.float32),
        jnp.zeros((length, kv_heads, per_kv, HD), jnp.float32),
    )
    for d in range(reach + 1):
        softmax_state, block = lax.optimization_barrier((softmax_state, gathered[d]))
        key_block = block[0].reshape(length, kv_heads, HD)
        value_block = block[1].reshape(length, kv_heads, HD)
        softmax_state = absorb(
            softmax_state, query_heads, key_block, value_block, block_mask(d), scaling
        )
    running, denominator, accumulated = softmax_state
    out_heads = (accumulated / denominator[..., None]).astype(jnp.bfloat16)
    log_total = running + jnp.log(denominator)
    row_dot = jnp.sum(grad_heads.astype(jnp.float32) * out_heads.astype(jnp.float32), axis=-1)

    query_acc = jnp.zeros((length, kv_heads, per_kv, HD), jnp.float32)
    order = [d for step, take in reversed(steps) for d in range(step + take - 1, step - 1, -1)]
    order.append(0)
    step_of = {step + take - 1 - (take - 1): (step, take) for step, take in steps}
    partials = {}
    arrivals = {}
    tied = {}
    for index, d in enumerate(order):
        waiting = tied.pop(index, None)
        if waiting is None:
            query_acc, block = lax.optimization_barrier((query_acc, gathered[d]))
        else:
            query_acc, block, got = lax.optimization_barrier((query_acc, gathered[d], arrivals[waiting]))
            arrivals[waiting] = got
        key_block = block[0].reshape(length, kv_heads, HD)
        value_block = block[1].reshape(length, kv_heads, HD)
        query_part, key_part, value_part = contrib(
            query_heads, grad_heads, log_total, row_dot, key_block, value_block,
            block_mask(d), scaling,
        )
        query_acc = query_acc + query_part
        partials[d] = jnp.stack((key_part.reshape(length, -1), value_part.reshape(length, -1)))
        if d in step_of:
            step, take = step_of[d]
            slots = list(range(step, step + take))
            for slot in slots:
                for wider, got in arrivals.items():
                    if slot < len(got):
                        partials[slot] = partials[slot] + got[slot].astype(jnp.float32)
            payload = jnp.stack([partials[slot] for slot in slots]).astype(jnp.bfloat16)
            arrivals[step] = shifted(payload, "seq", -step)
            if index + 2 < len(order):
                tied[index + 2] = step
    grad_sums = partials[0]
    for got in arrivals.values():
        grad_sums = grad_sums + got[0].astype(jnp.float32)

    return tuple(
        from_heads(
            [
                out_heads.reshape(length, -1),
                query_acc.astype(jnp.bfloat16).reshape(length, -1),
                grad_sums[0].astype(jnp.bfloat16),
                grad_sums[1].astype(jnp.bfloat16),
            ],
            groups,
        )
    )


def solution(mesh):
    return jax.shard_map(
        per_device,
        mesh=mesh,
        in_specs=(
            P(("seq", "tp"), None),
            P(("seq", "tp"), None),
            P(("seq", "tp"), None),
            P(("seq", "tp"), None),
            P(),
        ),
        out_specs=(
            P(("seq", "tp"), None),
            P(("seq", "tp"), None),
            P(("seq", "tp"), None),
            P(("seq", "tp"), None),
        ),
        check_vma=False,
    )
```

```python
import jax
import jax.numpy as jnp
from jax import lax
from jax.sharding import PartitionSpec as P

HD = 128
QH = 20
KVH = 4
LONG = 4096


def shifted(value, axis, by):
    peers = lax.axis_size(axis)
    pairs = [(i, i + by) for i in range(peers) if 0 <= i + by < peers]
    return lax.ppermute(value, axis, pairs)


def placed(first_row, row_count, doc_ends):
    position = first_row + jnp.arange(row_count, dtype=jnp.int32)
    segment = jnp.sum((position[:, None] >= doc_ends[None, :]).astype(jnp.int32), axis=1)
    return (position, segment)


def allowed(query_pos, query_seg, key_pos, key_seg):
    return (
        (key_pos[None, :] <= query_pos[:, None])
        & (key_pos[None, :] >= 0)
        & (key_seg[None, :] == query_seg[:, None])
    )


def absorb(softmax_state, query_heads, key_block, value_block, visible, scaling):
    running, denominator, accumulated = softmax_state
    scores = (
        jnp.einsum("bkgd,tkd->bkgt", query_heads, key_block, preferred_element_type=jnp.float32)
        * scaling
    )
    spread = visible[:, None, None, :]
    scores = jnp.where(spread, scores, -1e30)
    newest = jnp.maximum(running, jnp.max(scores, axis=-1))
    weight = jnp.where(spread, jnp.exp(scores - newest[..., None]), 0.0)
    shrink = jnp.exp(running - newest)
    denominator = denominator * shrink + jnp.sum(weight, axis=-1)
    accumulated = accumulated * shrink[..., None] + jnp.einsum(
        "bkgt,tkd->bkgd",
        weight.astype(jnp.bfloat16),
        value_block,
        preferred_element_type=jnp.float32,
    )
    return (newest, denominator, accumulated)


def contrib(query_heads, grad_heads, log_total, row_dot, key_block, value_block, visible, scaling):
    scores = (
        jnp.einsum("bkgd,tkd->bkgt", query_heads, key_block, preferred_element_type=jnp.float32)
        * scaling
    )
    spread = visible[:, None, None, :]
    scores = jnp.where(spread, scores, -1e30)
    probability = jnp.where(spread, jnp.exp(scores - log_total[..., None]), 0.0)
    value_part = jnp.einsum(
        "bkgt,bkgd->tkd",
        probability.astype(jnp.bfloat16),
        grad_heads,
        preferred_element_type=jnp.float32,
    )
    grad_prob = jnp.einsum(
        "bkgd,tkd->bkgt", grad_heads, value_block, preferred_element_type=jnp.float32
    )
    grad_score = (probability * (grad_prob - row_dot[..., None])).astype(jnp.bfloat16)
    query_part = (
        jnp.einsum("bkgt,tkd->bkgd", grad_score, key_block, preferred_element_type=jnp.float32)
        * scaling
    )
    key_part = (
        jnp.einsum("bkgt,bkgd->tkd", grad_score, query_heads, preferred_element_type=jnp.float32)
        * scaling
    )
    return (query_part, key_part, value_part)


def to_heads(arrays, groups):
    rows = arrays[0].shape[0]
    widths = [a.shape[1] // groups for a in arrays]
    joined = jnp.concatenate([a.reshape(rows, groups, -1) for a in arrays], axis=2)
    moved = lax.all_to_all(joined, "tp", split_axis=1, concat_axis=0, tiled=True)
    moved = moved.reshape(rows * groups, -1)
    pieces = []
    start = 0
    for w in widths:
        pieces.append(moved[:, start:start + w])
        start += w
    return pieces


def from_heads(arrays, groups):
    rows = arrays[0].shape[0] // groups
    widths = [a.shape[1] for a in arrays]
    joined = jnp.concatenate(arrays, axis=1).reshape(groups, rows, 1, -1)
    moved = lax.all_to_all(joined, "tp", split_axis=0, concat_axis=2, tiled=True)
    moved = moved.reshape(rows, groups, -1)
    pieces = []
    start = 0
    for w in widths:
        pieces.append(moved[:, :, start:start + w].reshape(rows, groups * w))
        start += w
    return pieces


def per_device(query_rows, key_rows, value_rows, out_grad, doc_lengths):
    per_kv = QH // KVH
    scaling = HD ** (-0.5)
    groups = lax.axis_size("tp")
    query_here, key_here, value_here = to_heads([query_rows, key_rows, value_rows], groups)
    length = query_here.shape[0]
    kv_heads = key_here.shape[1] // HD
    query_heads = query_here.reshape(length, kv_heads, per_kv, HD)
    seq_count = lax.axis_size("seq")
    position = lax.axis_index("seq")
    doc_ends = jnp.cumsum(doc_lengths)
    first_query = position * length
    query_pos, query_seg = placed(first_query, length, doc_ends)
    reach = min((length - 1 + LONG - 1) // length, seq_count - 1)

    key_value = jnp.stack((key_here, value_here))
    gathered = [key_value]
    while len(gathered) < reach + 1:
        step = len(gathered)
        take = min(step, reach + 1 - step)
        arrived = shifted(jnp.stack(gathered[:take]), "seq", step)
        gathered += [arrived[i] for i in range(take)]

    def block_mask(d):
        key_pos, key_seg = placed(first_query - d * length, length, doc_ends)
        return allowed(query_pos, query_seg, key_pos, key_seg)

    softmax_state = (
        jnp.full((length, kv_heads, per_kv), -1e30, jnp.float32),
        jnp.zeros((length, kv_heads, per_kv), jnp.float32),
        jnp.zeros((length, kv_heads, per_kv, HD), jnp.float32),
    )
    for d in range(reach + 1):
        softmax_state, block = lax.optimization_barrier((softmax_state, gathered[d]))
        key_block = block[0].reshape(length, kv_heads, HD)
        value_block = block[1].reshape(length, kv_heads, HD)
        softmax_state = absorb(
            softmax_state, query_heads, key_block, value_block, block_mask(d), scaling
        )
        if d == 0:
            out_grad, softmax_state = lax.optimization_barrier((out_grad, softmax_state))
            (grad_here,) = to_heads([out_grad], groups)
            grad_heads = grad_here.reshape(length, kv_heads, per_kv, HD)
    running, denominator, accumulated = softmax_state
    out_heads = (accumulated / denominator[..., None]).astype(jnp.bfloat16)
    log_total = running + jnp.log(denominator)
    row_dot = jnp.sum(grad_heads.astype(jnp.float32) * out_heads.astype(jnp.float32), axis=-1)

    query_acc = jnp.zeros((length, kv_heads, per_kv, HD), jnp.float32)
    sent = {}
    for d in range(reach, -1, -1):
        arrived = sent.pop(d + 3, None)
        if arrived is None:
            query_acc, block = lax.optimization_barrier((query_acc, gathered[d]))
        else:
            query_acc, block, arrived = lax.optimization_barrier((query_acc, gathered[d], arrived))
            sent[("in", d + 3)] = arrived
        key_block = block[0].reshape(length, kv_heads, HD)
        value_block = block[1].reshape(length, kv_heads, HD)
        query_part, key_part, value_part = contrib(
            query_heads, grad_heads, log_total, row_dot, key_block, value_block,
            block_mask(d), scaling,
        )
        query_acc = query_acc + query_part
        part = jnp.stack((key_part.reshape(length, -1), value_part.reshape(length, -1)))
        if d > 0:
            sent[d] = shifted(part.astype(jnp.bfloat16), "seq", -d)
        else:
            own = part
    grad_sums = own
    for received in sent.values():
        grad_sums = grad_sums + received.astype(jnp.float32)

    return tuple(
        from_heads(
            [
                out_heads.reshape(length, -1),
                query_acc.astype(jnp.bfloat16).reshape(length, -1),
                grad_sums[0].astype(jnp.bfloat16),
                grad_sums[1].astype(jnp.bfloat16),
            ],
            groups,
        )
    )


def solution(mesh):
    return jax.shard_map(
        per_device,
        mesh=mesh,
        in_specs=(
            P(("seq", "tp"), None),
            P(("seq", "tp"), None),
            P(("seq", "tp"), None),
            P(("seq", "tp"), None),
            P(),
        ),
        out_specs=(
            P(("seq", "tp"), None),
            P(("seq", "tp"), None),
            P(("seq", "tp"), None),
            P(("seq", "tp"), None),
        ),
        check_vma=False,
    )
```

```python
import jax
import jax.numpy as jnp
from jax import lax
from jax.sharding import PartitionSpec as P

HD = 128
QH = 20
KVH = 4
LONG = 4096


def shifted(value, axis, by):
    peers = lax.axis_size(axis)
    pairs = [(i, i + by) for i in range(peers) if 0 <= i + by < peers]
    return lax.ppermute(value, axis, pairs)


def placed(first_row, row_count, doc_ends):
    position = first_row + jnp.arange(row_count, dtype=jnp.int32)
    segment = jnp.sum((position[:, None] >= doc_ends[None, :]).astype(jnp.int32), axis=1)
    return (position, segment)


def allowed(query_pos, query_seg, key_pos, key_seg):
    return (
        (key_pos[None, :] <= query_pos[:, None])
        & (key_pos[None, :] >= 0)
        & (key_seg[None, :] == query_seg[:, None])
    )


def absorb(softmax_state, query_heads, key_block, value_block, visible, scaling):
    running, denominator, accumulated = softmax_state
    scores = (
        jnp.einsum("bkgd,tkd->bkgt", query_heads, key_block, preferred_element_type=jnp.float32)
        * scaling
    )
    spread = visible[:, None, None, :]
    scores = jnp.where(spread, scores, -1e30)
    newest = jnp.maximum(running, jnp.max(scores, axis=-1))
    weight = jnp.where(spread, jnp.exp(scores - newest[..., None]), 0.0)
    shrink = jnp.exp(running - newest)
    denominator = denominator * shrink + jnp.sum(weight, axis=-1)
    accumulated = accumulated * shrink[..., None] + jnp.einsum(
        "bkgt,tkd->bkgd",
        weight.astype(jnp.bfloat16),
        value_block,
        preferred_element_type=jnp.float32,
    )
    return (newest, denominator, accumulated)


def contrib(query_heads, grad_heads, log_total, row_dot, key_block, value_block, visible, scaling):
    scores = (
        jnp.einsum("bkgd,tkd->bkgt", query_heads, key_block, preferred_element_type=jnp.float32)
        * scaling
    )
    spread = visible[:, None, None, :]
    scores = jnp.where(spread, scores, -1e30)
    probability = jnp.where(spread, jnp.exp(scores - log_total[..., None]), 0.0)
    value_part = jnp.einsum(
        "bkgt,bkgd->tkd",
        probability.astype(jnp.bfloat16),
        grad_heads,
        preferred_element_type=jnp.float32,
    )
    grad_prob = jnp.einsum(
        "bkgd,tkd->bkgt", grad_heads, value_block, preferred_element_type=jnp.float32
    )
    grad_score = (probability * (grad_prob - row_dot[..., None])).astype(jnp.bfloat16)
    query_part = (
        jnp.einsum("bkgt,tkd->bkgd", grad_score, key_block, preferred_element_type=jnp.float32)
        * scaling
    )
    key_part = (
        jnp.einsum("bkgt,bkgd->tkd", grad_score, query_heads, preferred_element_type=jnp.float32)
        * scaling
    )
    return (query_part, key_part, value_part)


def to_heads(arrays, groups):
    rows = arrays[0].shape[0]
    widths = [a.shape[1] // groups for a in arrays]
    joined = jnp.concatenate([a.reshape(rows, groups, -1) for a in arrays], axis=2)
    moved = lax.all_to_all(joined, "tp", split_axis=1, concat_axis=0, tiled=True)
    moved = moved.reshape(rows * groups, -1)
    pieces = []
    start = 0
    for w in widths:
        pieces.append(moved[:, start:start + w])
        start += w
    return pieces


def from_heads(arrays, groups):
    rows = arrays[0].shape[0] // groups
    widths = [a.shape[1] for a in arrays]
    joined = jnp.concatenate(arrays, axis=1).reshape(groups, rows, 1, -1)
    moved = lax.all_to_all(joined, "tp", split_axis=0, concat_axis=2, tiled=True)
    moved = moved.reshape(rows, groups, -1)
    pieces = []
    start = 0
    for w in widths:
        pieces.append(moved[:, :, start:start + w].reshape(rows, groups * w))
        start += w
    return pieces


def per_device(query_rows, key_rows, value_rows, out_grad, doc_lengths):
    per_kv = QH // KVH
    scaling = HD ** (-0.5)
    groups = lax.axis_size("tp")
    query_here, key_here, value_here = to_heads([query_rows, key_rows, value_rows], groups)
    (grad_here,) = to_heads([out_grad], groups)
    length = query_here.shape[0]
    kv_heads = key_here.shape[1] // HD
    query_heads = query_here.reshape(length, kv_heads, per_kv, HD)
    grad_heads = grad_here.reshape(length, kv_heads, per_kv, HD)
    seq_count = lax.axis_size("seq")
    position = lax.axis_index("seq")
    doc_ends = jnp.cumsum(doc_lengths)
    first_query = position * length
    query_pos, query_seg = placed(first_query, length, doc_ends)
    reach = min((length - 1 + LONG - 1) // length, seq_count - 1)

    key_value = jnp.stack((key_here, value_here))
    gathered = [key_value]
    while len(gathered) < reach + 1:
        step = len(gathered)
        take = min(step, reach + 1 - step)
        arrived = shifted(jnp.stack(gathered[:take]), "seq", step)
        gathered += [arrived[i] for i in range(take)]

    doc_start = jnp.max(
        jnp.where(doc_ends[None, :] <= query_pos[:, None], doc_ends[None, :], 0), axis=1
    )

    def block_mask(d):
        key_pos = first_query - d * length + jnp.arange(length, dtype=jnp.int32)
        return (key_pos[None, :] >= doc_start[:, None]) & (key_pos[None, :] <= query_pos[:, None])

    softmax_state = (
        jnp.full((length, kv_heads, per_kv), -1e30, jnp.float32),
        jnp.zeros((length, kv_heads, per_kv), jnp.float32),
        jnp.zeros((length, kv_heads, per_kv, HD), jnp.float32),
    )
    for d in range(reach + 1):
        softmax_state, block = lax.optimization_barrier((softmax_state, gathered[d]))
        key_block = block[0].reshape(length, kv_heads, HD)
        value_block = block[1].reshape(length, kv_heads, HD)
        softmax_state = absorb(
            softmax_state, query_heads, key_block, value_block, block_mask(d), scaling
        )
    running, denominator, accumulated = softmax_state
    out_heads = (accumulated / denominator[..., None]).astype(jnp.bfloat16)
    log_total = running + jnp.log(denominator)
    row_dot = jnp.sum(grad_heads.astype(jnp.float32) * out_heads.astype(jnp.float32), axis=-1)

    query_acc = jnp.zeros((length, kv_heads, per_kv, HD), jnp.float32)
    sent = {}
    for d in range(reach, -1, -1):
        arrived = sent.pop(d + 3, None)
        if arrived is None:
            query_acc, block = lax.optimization_barrier((query_acc, gathered[d]))
        else:
            query_acc, block, arrived = lax.optimization_barrier((query_acc, gathered[d], arrived))
            sent[("in", d + 3)] = arrived
        key_block = block[0].reshape(length, kv_heads, HD)
        value_block = block[1].reshape(length, kv_heads, HD)
        query_part, key_part, value_part = contrib(
            query_heads, grad_heads, log_total, row_dot, key_block, value_block,
            block_mask(d), scaling,
        )
        query_acc = query_acc + query_part
        part = jnp.stack((key_part.reshape(length, -1), value_part.reshape(length, -1)))
        if d > 0:
            sent[d] = shifted(part.astype(jnp.bfloat16), "seq", -d)
        else:
            own = part
    grad_sums = own
    for received in sent.values():
        grad_sums = grad_sums + received.astype(jnp.float32)

    return tuple(
        from_heads(
            [
                out_heads.reshape(length, -1),
                query_acc.astype(jnp.bfloat16).reshape(length, -1),
                grad_sums[0].astype(jnp.bfloat16),
                grad_sums[1].astype(jnp.bfloat16),
            ],
            groups,
        )
    )


def solution(mesh):
    return jax.shard_map(
        per_device,
        mesh=mesh,
        in_specs=(
            P(("seq", "tp"), None),
            P(("seq", "tp"), None),
            P(("seq", "tp"), None),
            P(("seq", "tp"), None),
            P(),
        ),
        out_specs=(
            P(("seq", "tp"), None),
            P(("seq", "tp"), None),
            P(("seq", "tp"), None),
            P(("seq", "tp"), None),
        ),
        check_vma=False,
    )
```

```python
import jax
import jax.numpy as jnp
from jax import lax
from jax.sharding import PartitionSpec as P

HD = 128
QH = 20
KVH = 4
LONG = 4096


def shifted(value, axis, by):
    peers = lax.axis_size(axis)
    pairs = [(i, i + by) for i in range(peers) if 0 <= i + by < peers]
    return lax.ppermute(value, axis, pairs)


def placed(first_row, row_count, doc_ends):
    position = first_row + jnp.arange(row_count, dtype=jnp.int32)
    segment = jnp.sum((position[:, None] >= doc_ends[None, :]).astype(jnp.int32), axis=1)
    return (position, segment)


def allowed(query_pos, query_seg, key_pos, key_seg):
    return (
        (key_pos[None, :] <= query_pos[:, None])
        & (key_pos[None, :] >= 0)
        & (key_seg[None, :] == query_seg[:, None])
    )


def absorb(softmax_state, query_heads, key_block, value_block, visible, scaling):
    running, denominator, accumulated = softmax_state
    scores = (
        jnp.einsum("bkgd,tkd->bkgt", query_heads, key_block, preferred_element_type=jnp.float32)
        * scaling
    )
    spread = visible[:, None, None, :]
    scores = jnp.where(spread, scores, -1e30)
    newest = jnp.maximum(running, jnp.max(scores, axis=-1))
    weight = jnp.where(spread, jnp.exp(scores - newest[..., None]), 0.0)
    shrink = jnp.exp(running - newest)
    denominator = denominator * shrink + jnp.sum(weight, axis=-1)
    accumulated = accumulated * shrink[..., None] + jnp.einsum(
        "bkgt,tkd->bkgd",
        weight.astype(jnp.bfloat16),
        value_block,
        preferred_element_type=jnp.float32,
    )
    return (newest, denominator, accumulated)


def contrib(query_heads, grad_heads, log_total, row_dot, key_block, value_block, visible, scaling):
    scores = (
        jnp.einsum("bkgd,tkd->bkgt", query_heads, key_block, preferred_element_type=jnp.float32)
        * scaling
    )
    spread = visible[:, None, None, :]
    scores = jnp.where(spread, scores, -1e30)
    probability = jnp.where(spread, jnp.exp(scores - log_total[..., None]), 0.0)
    value_part = jnp.einsum(
        "bkgt,bkgd->tkd",
        probability.astype(jnp.bfloat16),
        grad_heads,
        preferred_element_type=jnp.float32,
    )
    grad_prob = jnp.einsum(
        "bkgd,tkd->bkgt", grad_heads, value_block, preferred_element_type=jnp.float32
    )
    grad_score = (probability * (grad_prob - row_dot[..., None])).astype(jnp.bfloat16)
    query_part = (
        jnp.einsum("bkgt,tkd->bkgd", grad_score, key_block, preferred_element_type=jnp.float32)
        * scaling
    )
    key_part = (
        jnp.einsum("bkgt,bkgd->tkd", grad_score, query_heads, preferred_element_type=jnp.float32)
        * scaling
    )
    return (query_part, key_part, value_part)


def to_heads(arrays, groups):
    rows = arrays[0].shape[0]
    widths = [a.shape[1] // groups for a in arrays]
    joined = jnp.concatenate([a.reshape(rows, groups, -1) for a in arrays], axis=2)
    moved = lax.all_to_all(joined, "tp", split_axis=1, concat_axis=0, tiled=True)
    moved = moved.reshape(rows * groups, -1)
    pieces = []
    start = 0
    for w in widths:
        pieces.append(moved[:, start:start + w])
        start += w
    return pieces


def from_heads(arrays, groups):
    rows = arrays[0].shape[0] // groups
    widths = [a.shape[1] for a in arrays]
    joined = jnp.concatenate(arrays, axis=1).reshape(groups, rows, 1, -1)
    moved = lax.all_to_all(joined, "tp", split_axis=0, concat_axis=2, tiled=True)
    moved = moved.reshape(rows, groups, -1)
    pieces = []
    start = 0
    for w in widths:
        pieces.append(moved[:, :, start:start + w].reshape(rows, groups * w))
        start += w
    return pieces


def per_device(query_rows, key_rows, value_rows, out_grad, doc_lengths):
    per_kv = QH // KVH
    scaling = HD ** (-0.5)
    groups = lax.axis_size("tp")
    query_here, key_here, value_here = to_heads([query_rows, key_rows, value_rows], groups)
    (grad_here,) = to_heads([out_grad], groups)
    length = query_here.shape[0]
    kv_heads = key_here.shape[1] // HD
    query_heads = query_here.reshape(length, kv_heads, per_kv, HD)
    grad_heads = grad_here.reshape(length, kv_heads, per_kv, HD)
    seq_count = lax.axis_size("seq")
    position = lax.axis_index("seq")
    doc_ends = jnp.cumsum(doc_lengths)
    first_query = position * length
    query_pos, query_seg = placed(first_query, length, doc_ends)
    reach = min((length - 1 + LONG - 1) // length, seq_count - 1)

    key_value = jnp.stack((key_here, value_here))
    gathered = [key_value]
    steps = []
    while len(gathered) < reach + 1:
        step = len(gathered)
        take = min(step, reach + 1 - step)
        arrived = shifted(jnp.stack(gathered[:take]), "seq", step)
        gathered += [arrived[i] for i in range(take)]
        steps.append((step, take))

    doc_start = jnp.max(
        jnp.where(doc_ends[None, :] <= query_pos[:, None], doc_ends[None, :], 0), axis=1
    )

    def block_mask(ds):
        key_pos = jnp.concatenate(
            [first_query - d * length + jnp.arange(length, dtype=jnp.int32) for d in ds]
        )
        return (key_pos[None, :] >= doc_start[:, None]) & (key_pos[None, :] <= query_pos[:, None])

    def joined(blocks):
        key_block = jnp.concatenate([b[0] for b in blocks], axis=0)
        value_block = jnp.concatenate([b[1] for b in blocks], axis=0)
        rows = key_block.shape[0]
        return key_block.reshape(rows, kv_heads, HD), value_block.reshape(rows, kv_heads, HD)

    forward_groups = [(0,)]
    for step, take in steps:
        slots = list(range(step, step + take))
        forward_groups += [tuple(slots[i:i + 2]) for i in range(0, take, 2)]

    softmax_state = (
        jnp.full((length, kv_heads, per_kv), -1e30, jnp.float32),
        jnp.zeros((length, kv_heads, per_kv), jnp.float32),
        jnp.zeros((length, kv_heads, per_kv, HD), jnp.float32),
    )
    for ds in forward_groups:
        softmax_state, blocks = lax.optimization_barrier(
            (softmax_state, [gathered[d] for d in ds])
        )
        key_block, value_block = joined(blocks)
        softmax_state = absorb(
            softmax_state, query_heads, key_block, value_block, block_mask(ds), scaling
        )
    running, denominator, accumulated = softmax_state
    out_heads = (accumulated / denominator[..., None]).astype(jnp.bfloat16)
    log_total = running + jnp.log(denominator)
    row_dot = jnp.sum(grad_heads.astype(jnp.float32) * out_heads.astype(jnp.float32), axis=-1)

    backward_groups = [tuple(reversed(g)) for g in reversed(forward_groups)]
    query_acc = jnp.zeros((length, kv_heads, per_kv, HD), jnp.float32)
    sent = {}
    pending = {}
    for index, ds in enumerate(backward_groups):
        waiting = pending.pop(index, [])
        query_acc, blocks, got = lax.optimization_barrier(
            (query_acc, [gathered[d] for d in ds], [sent[d] for d in waiting])
        )
        for d, value in zip(waiting, got):
            sent[d] = value
        key_block, value_block = joined(blocks)
        query_part, key_part, value_part = contrib(
            query_heads, grad_heads, log_total, row_dot, key_block, value_block,
            block_mask(ds), scaling,
        )
        query_acc = query_acc + query_part
        for j, d in enumerate(ds):
            part = jnp.stack(
                (
                    key_part[j * length:(j + 1) * length].reshape(length, -1),
                    value_part[j * length:(j + 1) * length].reshape(length, -1),
                )
            )
            if d > 0:
                sent[d] = shifted(part.astype(jnp.bfloat16), "seq", -d)
                if index + 2 < len(backward_groups):
                    pending.setdefault(index + 2, []).append(d)
            else:
                own = part
    grad_sums = own
    for received in sent.values():
        grad_sums = grad_sums + received.astype(jnp.float32)

    return tuple(
        from_heads(
            [
                out_heads.reshape(length, -1),
                query_acc.astype(jnp.bfloat16).reshape(length, -1),
                grad_sums[0].astype(jnp.bfloat16),
                grad_sums[1].astype(jnp.bfloat16),
            ],
            groups,
        )
    )


def solution(mesh):
    return jax.shard_map(
        per_device,
        mesh=mesh,
        in_specs=(
            P(("seq", "tp"), None),
            P(("seq", "tp"), None),
            P(("seq", "tp"), None),
            P(("seq", "tp"), None),
            P(),
        ),
        out_specs=(
            P(("seq", "tp"), None),
            P(("seq", "tp"), None),
            P(("seq", "tp"), None),
            P(("seq", "tp"), None),
        ),
        check_vma=False,
    )
```

```python
import jax
import jax.numpy as jnp
from jax import lax
from jax.sharding import PartitionSpec as P

HD = 128
QH = 20
KVH = 4
LONG = 4096


def shifted(value, axis, by):
    peers = lax.axis_size(axis)
    pairs = [(i, i + by) for i in range(peers) if 0 <= i + by < peers]
    return lax.ppermute(value, axis, pairs)


def placed(first_row, row_count, doc_ends):
    position = first_row + jnp.arange(row_count, dtype=jnp.int32)
    segment = jnp.sum((position[:, None] >= doc_ends[None, :]).astype(jnp.int32), axis=1)
    return (position, segment)


def allowed(query_pos, query_seg, key_pos, key_seg):
    return (
        (key_pos[None, :] <= query_pos[:, None])
        & (key_pos[None, :] >= 0)
        & (key_seg[None, :] == query_seg[:, None])
    )


def absorb(softmax_state, query_heads, key_block, value_block, visible, scaling):
    running, denominator, accumulated = softmax_state
    scores = (
        jnp.einsum("bkgd,tkd->bkgt", query_heads, key_block, preferred_element_type=jnp.float32)
        * scaling
    )
    spread = visible[:, None, None, :]
    scores = jnp.where(spread, scores, -1e30)
    newest = jnp.maximum(running, jnp.max(scores, axis=-1))
    weight = lax.optimization_barrier(jnp.where(spread, jnp.exp(scores - newest[..., None]), 0.0))
    shrink = jnp.exp(running - newest)
    denominator = denominator * shrink + jnp.sum(weight, axis=-1)
    accumulated = accumulated * shrink[..., None] + jnp.einsum(
        "bkgt,tkd->bkgd",
        weight.astype(jnp.bfloat16),
        value_block,
        preferred_element_type=jnp.float32,
    )
    return (newest, denominator, accumulated)


def contrib(query_heads, grad_heads, log_total, row_dot, key_block, value_block, visible, scaling):
    scores = (
        jnp.einsum("bkgd,tkd->bkgt", query_heads, key_block, preferred_element_type=jnp.float32)
        * scaling
    )
    spread = visible[:, None, None, :]
    scores = jnp.where(spread, scores, -1e30)
    probability = lax.optimization_barrier(
        jnp.where(spread, jnp.exp(scores - log_total[..., None]), 0.0)
    )
    value_part = jnp.einsum(
        "bkgt,bkgd->tkd",
        probability.astype(jnp.bfloat16),
        grad_heads,
        preferred_element_type=jnp.float32,
    )
    grad_prob = jnp.einsum(
        "bkgd,tkd->bkgt", grad_heads, value_block, preferred_element_type=jnp.float32
    )
    grad_score = (probability * (grad_prob - row_dot[..., None])).astype(jnp.bfloat16)
    query_part = (
        jnp.einsum("bkgt,tkd->bkgd", grad_score, key_block, preferred_element_type=jnp.float32)
        * scaling
    )
    key_part = (
        jnp.einsum("bkgt,bkgd->tkd", grad_score, query_heads, preferred_element_type=jnp.float32)
        * scaling
    )
    return (query_part, key_part, value_part)


def to_heads(arrays, groups):
    rows = arrays[0].shape[0]
    widths = [a.shape[1] // groups for a in arrays]
    joined = jnp.concatenate([a.reshape(rows, groups, -1) for a in arrays], axis=2)
    moved = lax.all_to_all(joined, "tp", split_axis=1, concat_axis=0, tiled=True)
    moved = moved.reshape(rows * groups, -1)
    pieces = []
    start = 0
    for w in widths:
        pieces.append(moved[:, start:start + w])
        start += w
    return pieces


def from_heads(arrays, groups):
    rows = arrays[0].shape[0] // groups
    widths = [a.shape[1] for a in arrays]
    joined = jnp.concatenate(arrays, axis=1).reshape(groups, rows, 1, -1)
    moved = lax.all_to_all(joined, "tp", split_axis=0, concat_axis=2, tiled=True)
    moved = moved.reshape(rows, groups, -1)
    pieces = []
    start = 0
    for w in widths:
        pieces.append(moved[:, :, start:start + w].reshape(rows, groups * w))
        start += w
    return pieces


def per_device(query_rows, key_rows, value_rows, out_grad, doc_lengths):
    per_kv = QH // KVH
    scaling = HD ** (-0.5)
    groups = lax.axis_size("tp")
    query_here, key_here, value_here = to_heads([query_rows, key_rows, value_rows], groups)
    (grad_here,) = to_heads([out_grad], groups)
    length = query_here.shape[0]
    kv_heads = key_here.shape[1] // HD
    query_heads = query_here.reshape(length, kv_heads, per_kv, HD)
    grad_heads = grad_here.reshape(length, kv_heads, per_kv, HD)
    seq_count = lax.axis_size("seq")
    position = lax.axis_index("seq")
    doc_ends = jnp.cumsum(doc_lengths)
    first_query = position * length
    query_pos, query_seg = placed(first_query, length, doc_ends)
    reach = min((length - 1 + LONG - 1) // length, seq_count - 1)

    key_value = jnp.stack((key_here, value_here))
    gathered = [key_value]
    while len(gathered) < reach + 1:
        step = len(gathered)
        take = min(step, reach + 1 - step)
        arrived = shifted(jnp.stack(gathered[:take]), "seq", step)
        gathered += [arrived[i] for i in range(take)]

    doc_start = jnp.max(
        jnp.where(doc_ends[None, :] <= query_pos[:, None], doc_ends[None, :], 0), axis=1
    )

    def block_mask(d):
        key_pos = first_query - d * length + jnp.arange(length, dtype=jnp.int32)
        return (key_pos[None, :] >= doc_start[:, None]) & (key_pos[None, :] <= query_pos[:, None])

    softmax_state = (
        jnp.full((length, kv_heads, per_kv), -1e30, jnp.float32),
        jnp.zeros((length, kv_heads, per_kv), jnp.float32),
        jnp.zeros((length, kv_heads, per_kv, HD), jnp.float32),
    )
    for d in range(reach + 1):
        softmax_state, block = lax.optimization_barrier((softmax_state, gathered[d]))
        key_block = block[0].reshape(length, kv_heads, HD)
        value_block = block[1].reshape(length, kv_heads, HD)
        softmax_state = absorb(
            softmax_state, query_heads, key_block, value_block, block_mask(d), scaling
        )
    running, denominator, accumulated = softmax_state
    out_heads = (accumulated / denominator[..., None]).astype(jnp.bfloat16)
    log_total = running + jnp.log(denominator)
    row_dot = jnp.sum(grad_heads.astype(jnp.float32) * out_heads.astype(jnp.float32), axis=-1)

    query_acc = jnp.zeros((length, kv_heads, per_kv, HD), jnp.float32)
    sent = {}
    for d in range(reach, -1, -1):
        arrived = sent.pop(d + 3, None)
        if arrived is None:
            query_acc, block = lax.optimization_barrier((query_acc, gathered[d]))
        else:
            query_acc, block, arrived = lax.optimization_barrier((query_acc, gathered[d], arrived))
            sent[("in", d + 3)] = arrived
        key_block = block[0].reshape(length, kv_heads, HD)
        value_block = block[1].reshape(length, kv_heads, HD)
        query_part, key_part, value_part = contrib(
            query_heads, grad_heads, log_total, row_dot, key_block, value_block,
            block_mask(d), scaling,
        )
        query_acc = query_acc + query_part
        part = jnp.stack((key_part.reshape(length, -1), value_part.reshape(length, -1)))
        if d > 0:
            sent[d] = shifted(part.astype(jnp.bfloat16), "seq", -d)
        else:
            own = part
    grad_sums = own
    for received in sent.values():
        grad_sums = grad_sums + received.astype(jnp.float32)

    return tuple(
        from_heads(
            [
                out_heads.reshape(length, -1),
                query_acc.astype(jnp.bfloat16).reshape(length, -1),
                grad_sums[0].astype(jnp.bfloat16),
                grad_sums[1].astype(jnp.bfloat16),
            ],
            groups,
        )
    )


def solution(mesh):
    return jax.shard_map(
        per_device,
        mesh=mesh,
        in_specs=(
            P(("seq", "tp"), None),
            P(("seq", "tp"), None),
            P(("seq", "tp"), None),
            P(("seq", "tp"), None),
            P(),
        ),
        out_specs=(
            P(("seq", "tp"), None),
            P(("seq", "tp"), None),
            P(("seq", "tp"), None),
            P(("seq", "tp"), None),
        ),
        check_vma=False,
    )
```

```python
import jax
import jax.numpy as jnp
from jax import lax
from jax.sharding import PartitionSpec as P

HD = 128
QH = 20
KVH = 4
LONG = 4096


def shifted(value, axis, by):
    peers = lax.axis_size(axis)
    pairs = [(i, i + by) for i in range(peers) if 0 <= i + by < peers]
    return lax.ppermute(value, axis, pairs)


def placed(first_row, row_count, doc_ends):
    position = first_row + jnp.arange(row_count, dtype=jnp.int32)
    segment = jnp.sum((position[:, None] >= doc_ends[None, :]).astype(jnp.int32), axis=1)
    return (position, segment)


def allowed(query_pos, query_seg, key_pos, key_seg):
    return (
        (key_pos[None, :] <= query_pos[:, None])
        & (key_pos[None, :] >= 0)
        & (key_seg[None, :] == query_seg[:, None])
    )


def absorb(softmax_state, query_heads, key_block, value_block, visible, scaling):
    running, denominator, accumulated = softmax_state
    scores = (
        jnp.einsum("bkgd,tkd->bkgt", query_heads, key_block, preferred_element_type=jnp.float32)
        * scaling
    )
    spread = visible[:, None, None, :]
    scores = jnp.where(spread, scores, -1e30)
    newest = jnp.maximum(running, jnp.max(scores, axis=-1))
    weight = jnp.where(spread, jnp.exp(scores - newest[..., None]), 0.0)
    shrink = jnp.exp(running - newest)
    denominator = denominator * shrink + jnp.sum(weight, axis=-1)
    accumulated = accumulated * shrink[..., None] + jnp.einsum(
        "bkgt,tkd->bkgd",
        weight.astype(jnp.bfloat16),
        value_block,
        preferred_element_type=jnp.float32,
    )
    return (newest, denominator, accumulated)


def contrib(query_heads, grad_heads, log_total, row_dot, key_block, value_block, visible, scaling):
    scores = (
        jnp.einsum("bkgd,tkd->bkgt", query_heads, key_block, preferred_element_type=jnp.float32)
        * scaling
    )
    spread = visible[:, None, None, :]
    scores = jnp.where(spread, scores, -1e30)
    probability = jnp.where(spread, jnp.exp(scores - log_total[..., None]), 0.0)
    value_part = jnp.einsum(
        "bkgt,bkgd->tkd",
        probability.astype(jnp.bfloat16),
        grad_heads,
        preferred_element_type=jnp.float32,
    )
    grad_prob = jnp.einsum(
        "bkgd,tkd->bkgt", grad_heads, value_block, preferred_element_type=jnp.float32
    )
    grad_score = (probability * (grad_prob - row_dot[..., None])).astype(jnp.bfloat16)
    query_part = (
        jnp.einsum("bkgt,tkd->bkgd", grad_score, key_block, preferred_element_type=jnp.float32)
        * scaling
    )
    key_part = (
        jnp.einsum("bkgt,bkgd->tkd", grad_score, query_heads, preferred_element_type=jnp.float32)
        * scaling
    )
    return (query_part, key_part, value_part)


def to_heads(arrays, groups):
    rows = arrays[0].shape[0]
    widths = [a.shape[1] // groups for a in arrays]
    joined = jnp.concatenate([a.reshape(rows, groups, -1) for a in arrays], axis=2)
    moved = lax.all_to_all(joined, "tp", split_axis=1, concat_axis=0, tiled=True)
    moved = moved.reshape(rows * groups, -1)
    pieces = []
    start = 0
    for w in widths:
        pieces.append(moved[:, start:start + w])
        start += w
    return pieces


def from_heads(arrays, groups):
    rows = arrays[0].shape[0] // groups
    widths = [a.shape[1] for a in arrays]
    joined = jnp.concatenate(arrays, axis=1).reshape(groups, rows, 1, -1)
    moved = lax.all_to_all(joined, "tp", split_axis=0, concat_axis=2, tiled=True)
    moved = moved.reshape(rows, groups, -1)
    pieces = []
    start = 0
    for w in widths:
        pieces.append(moved[:, :, start:start + w].reshape(rows, groups * w))
        start += w
    return pieces


def per_device(query_rows, key_rows, value_rows, out_grad, doc_lengths):
    per_kv = QH // KVH
    scaling = HD ** (-0.5)
    groups = lax.axis_size("tp")
    query_here, key_here, value_here = to_heads([query_rows, key_rows, value_rows], groups)
    (grad_here,) = to_heads([out_grad], groups)
    length = query_here.shape[0]
    kv_heads = key_here.shape[1] // HD
    query_heads = query_here.reshape(length, kv_heads, per_kv, HD)
    grad_heads = grad_here.reshape(length, kv_heads, per_kv, HD)
    seq_count = lax.axis_size("seq")
    position = lax.axis_index("seq")
    doc_ends = jnp.cumsum(doc_lengths)
    first_query = position * length
    query_pos, query_seg = placed(first_query, length, doc_ends)
    reach = min((length - 1 + LONG - 1) // length, seq_count - 1)

    key_value = jnp.stack((key_here, value_here))
    gathered = [key_value]
    while len(gathered) < reach + 1:
        step = len(gathered)
        take = min(step, reach + 1 - step)
        arrived = shifted(jnp.stack(gathered[:take]), "seq", step)
        gathered += [arrived[i] for i in range(take)]

    doc_start = jnp.max(
        jnp.where(doc_ends[None, :] <= query_pos[:, None], doc_ends[None, :], 0), axis=1
    )

    def block_mask(d):
        key_pos = first_query - d * length + jnp.arange(length, dtype=jnp.int32)
        return (key_pos[None, :] >= doc_start[:, None]) & (key_pos[None, :] <= query_pos[:, None])

    softmax_state = (
        jnp.full((length, kv_heads, per_kv), -1e30, jnp.float32),
        jnp.zeros((length, kv_heads, per_kv), jnp.float32),
        jnp.zeros((length, kv_heads, per_kv, HD), jnp.float32),
    )
    for d in range(reach + 1):
        softmax_state, block = lax.optimization_barrier((softmax_state, gathered[d]))
        key_block = block[0].reshape(length, kv_heads, HD)
        value_block = block[1].reshape(length, kv_heads, HD)
        softmax_state = absorb(
            softmax_state, query_heads, key_block, value_block, block_mask(d), scaling
        )
    running, denominator, accumulated = softmax_state
    out_heads = (accumulated / denominator[..., None]).astype(jnp.bfloat16)
    log_total = running + jnp.log(denominator)
    row_dot = jnp.sum(grad_heads.astype(jnp.float32) * out_heads.astype(jnp.float32), axis=-1)

    query_acc = jnp.zeros((length, kv_heads, per_kv, HD), jnp.float32)
    sent = {}
    for d in range(reach, -1, -1):
        arrived = sent.pop(d + 4, None)
        if arrived is None:
            query_acc, block = lax.optimization_barrier((query_acc, gathered[d]))
        else:
            query_acc, block, arrived = lax.optimization_barrier((query_acc, gathered[d], arrived))
            sent[("in", d + 4)] = arrived
        key_block = block[0].reshape(length, kv_heads, HD)
        value_block = block[1].reshape(length, kv_heads, HD)
        query_part, key_part, value_part = contrib(
            query_heads, grad_heads, log_total, row_dot, key_block, value_block,
            block_mask(d), scaling,
        )
        query_acc = query_acc + query_part
        part = jnp.stack((key_part.reshape(length, -1), value_part.reshape(length, -1)))
        if d > 0:
            sent[d] = shifted(part.astype(jnp.bfloat16), "seq", -d)
        else:
            own = part
    grad_sums = own
    for received in sent.values():
        grad_sums = grad_sums + received.astype(jnp.float32)

    return tuple(
        from_heads(
            [
                out_heads.reshape(length, -1),
                query_acc.astype(jnp.bfloat16).reshape(length, -1),
                grad_sums[0].astype(jnp.bfloat16),
                grad_sums[1].astype(jnp.bfloat16),
            ],
            groups,
        )
    )


def solution(mesh):
    return jax.shard_map(
        per_device,
        mesh=mesh,
        in_specs=(
            P(("seq", "tp"), None),
            P(("seq", "tp"), None),
            P(("seq", "tp"), None),
            P(("seq", "tp"), None),
            P(),
        ),
        out_specs=(
            P(("seq", "tp"), None),
            P(("seq", "tp"), None),
            P(("seq", "tp"), None),
            P(("seq", "tp"), None),
        ),
        check_vma=False,
    )
```

```python
import jax
import jax.numpy as jnp
from jax import lax
from jax.sharding import PartitionSpec as P

HD = 128
QH = 20
KVH = 4
LONG = 4096


def shifted(value, axis, by):
    peers = lax.axis_size(axis)
    pairs = [(i, i + by) for i in range(peers) if 0 <= i + by < peers]
    return lax.ppermute(value, axis, pairs)


def placed(first_row, row_count, doc_ends):
    position = first_row + jnp.arange(row_count, dtype=jnp.int32)
    segment = jnp.sum((position[:, None] >= doc_ends[None, :]).astype(jnp.int32), axis=1)
    return (position, segment)


def allowed(query_pos, query_seg, key_pos, key_seg):
    return (
        (key_pos[None, :] <= query_pos[:, None])
        & (key_pos[None, :] >= 0)
        & (key_seg[None, :] == query_seg[:, None])
    )


def absorb(softmax_state, query_heads, key_block, value_block, visible, scaling):
    running, denominator, accumulated = softmax_state
    scores = (
        jnp.einsum("bkgd,tkd->bkgt", query_heads, key_block, preferred_element_type=jnp.float32)
        * scaling
    )
    spread = visible[:, None, None, :]
    scores = jnp.where(spread, scores, -1e30)
    newest = jnp.maximum(running, jnp.max(scores, axis=-1))
    weight = jnp.where(spread, jnp.exp(scores - newest[..., None]), 0.0)
    shrink = jnp.exp(running - newest)
    denominator = denominator * shrink + jnp.sum(weight, axis=-1)
    accumulated = accumulated * shrink[..., None] + jnp.einsum(
        "bkgt,tkd->bkgd",
        weight.astype(jnp.bfloat16),
        value_block,
        preferred_element_type=jnp.float32,
    )
    return (newest, denominator, accumulated)


def contrib(query_heads, grad_heads, log_total, row_dot, key_block, value_block, visible, scaling):
    scores = (
        jnp.einsum("bkgd,tkd->bkgt", query_heads, key_block, preferred_element_type=jnp.float32)
        * scaling
    )
    spread = visible[:, None, None, :]
    scores = jnp.where(spread, scores, -1e30)
    probability = jnp.where(spread, jnp.exp(scores - log_total[..., None]), 0.0)
    value_part = jnp.einsum(
        "bkgt,bkgd->tkd",
        probability.astype(jnp.bfloat16),
        grad_heads,
        preferred_element_type=jnp.float32,
    )
    grad_prob = jnp.einsum(
        "bkgd,tkd->bkgt", grad_heads, value_block, preferred_element_type=jnp.float32
    )
    grad_score = (probability * (grad_prob - row_dot[..., None])).astype(jnp.bfloat16)
    query_part = (
        jnp.einsum("bkgt,tkd->bkgd", grad_score, key_block, preferred_element_type=jnp.float32)
        * scaling
    )
    key_part = (
        jnp.einsum("bkgt,bkgd->tkd", grad_score, query_heads, preferred_element_type=jnp.float32)
        * scaling
    )
    return (query_part, key_part, value_part)


def to_heads(arrays, groups):
    rows = arrays[0].shape[0]
    widths = [a.shape[1] // groups for a in arrays]
    joined = jnp.concatenate([a.reshape(rows, groups, -1) for a in arrays], axis=2)
    moved = lax.all_to_all(joined, "tp", split_axis=1, concat_axis=0, tiled=True)
    moved = moved.reshape(rows * groups, -1)
    pieces = []
    start = 0
    for w in widths:
        pieces.append(moved[:, start:start + w])
        start += w
    return pieces


def from_heads(arrays, groups):
    rows = arrays[0].shape[0] // groups
    widths = [a.shape[1] for a in arrays]
    joined = jnp.concatenate(arrays, axis=1).reshape(groups, rows, 1, -1)
    moved = lax.all_to_all(joined, "tp", split_axis=0, concat_axis=2, tiled=True)
    moved = moved.reshape(rows, groups, -1)
    pieces = []
    start = 0
    for w in widths:
        pieces.append(moved[:, :, start:start + w].reshape(rows, groups * w))
        start += w
    return pieces


def per_device(query_rows, key_rows, value_rows, out_grad, doc_lengths):
    per_kv = QH // KVH
    scaling = HD ** (-0.5)
    groups = lax.axis_size("tp")
    query_here, key_here, value_here = to_heads([query_rows, key_rows, value_rows], groups)
    (grad_here,) = to_heads([out_grad], groups)
    length = query_here.shape[0]
    kv_heads = key_here.shape[1] // HD
    query_heads = query_here.reshape(length, kv_heads, per_kv, HD)
    grad_heads = grad_here.reshape(length, kv_heads, per_kv, HD)
    seq_count = lax.axis_size("seq")
    position = lax.axis_index("seq")
    doc_ends = jnp.cumsum(doc_lengths)
    first_query = position * length
    query_pos, query_seg = placed(first_query, length, doc_ends)
    reach = min((length - 1 + LONG - 1) // length, seq_count - 1)

    key_value = jnp.stack((key_here, value_here))
    gathered = [key_value]
    while len(gathered) < reach + 1:
        step = len(gathered)
        take = min(step, reach + 1 - step)
        arrived = shifted(jnp.stack(gathered[:take]), "seq", step)
        gathered += [arrived[i] for i in range(take)]

    doc_start = jnp.max(
        jnp.where(doc_ends[None, :] <= query_pos[:, None], doc_ends[None, :], 0), axis=1
    )

    def block_mask(d):
        key_pos = first_query - d * length + jnp.arange(length, dtype=jnp.int32)
        return (key_pos[None, :] >= doc_start[:, None]) & (key_pos[None, :] <= query_pos[:, None])

    softmax_state = (
        jnp.full((length, kv_heads, per_kv), -1e30, jnp.float32),
        jnp.zeros((length, kv_heads, per_kv), jnp.float32),
        jnp.zeros((length, kv_heads, per_kv, HD), jnp.float32),
    )
    for d in range(reach + 1):
        softmax_state, block = lax.optimization_barrier((softmax_state, gathered[d]))
        key_block = block[0].reshape(length, kv_heads, HD)
        value_block = block[1].reshape(length, kv_heads, HD)
        softmax_state = absorb(
            softmax_state, query_heads, key_block, value_block, block_mask(d), scaling
        )
    running, denominator, accumulated = softmax_state
    out_heads = (accumulated / denominator[..., None]).astype(jnp.bfloat16)
    log_total = running + jnp.log(denominator)
    row_dot = jnp.sum(grad_heads.astype(jnp.float32) * out_heads.astype(jnp.float32), axis=-1)

    query_acc = jnp.zeros((length, kv_heads, per_kv, HD), jnp.float32)
    sent = {}
    for d in range(reach, -1, -1):
        arrived = sent.pop(d + 2, None)
        if arrived is None:
            query_acc, block = lax.optimization_barrier((query_acc, gathered[d]))
        else:
            query_acc, block, arrived = lax.optimization_barrier((query_acc, gathered[d], arrived))
            sent[("in", d + 2)] = arrived
        key_block = block[0].reshape(length, kv_heads, HD)
        value_block = block[1].reshape(length, kv_heads, HD)
        query_part, key_part, value_part = contrib(
            query_heads, grad_heads, log_total, row_dot, key_block, value_block,
            block_mask(d), scaling,
        )
        query_acc = query_acc + query_part
        part = jnp.stack((key_part.reshape(length, -1), value_part.reshape(length, -1)))
        if d > 0:
            sent[d] = shifted(part.astype(jnp.bfloat16), "seq", -d)
        else:
            own = part
    grad_sums = own
    for received in sent.values():
        grad_sums = grad_sums + received.astype(jnp.float32)

    return tuple(
        from_heads(
            [
                out_heads.reshape(length, -1),
                query_acc.astype(jnp.bfloat16).reshape(length, -1),
                grad_sums[0].astype(jnp.bfloat16),
                grad_sums[1].astype(jnp.bfloat16),
            ],
            groups,
        )
    )


def solution(mesh):
    return jax.shard_map(
        per_device,
        mesh=mesh,
        in_specs=(
            P(("seq", "tp"), None),
            P(("seq", "tp"), None),
            P(("seq", "tp"), None),
            P(("seq", "tp"), None),
            P(),
        ),
        out_specs=(
            P(("seq", "tp"), None),
            P(("seq", "tp"), None),
            P(("seq", "tp"), None),
            P(("seq", "tp"), None),
        ),
        check_vma=False,
    )
```

```python
import jax
import jax.numpy as jnp
from jax import lax
from jax.sharding import PartitionSpec as P

HD = 128
QH = 20
KVH = 4
LONG = 4096


def shifted(value, axis, by):
    peers = lax.axis_size(axis)
    pairs = [(i, i + by) for i in range(peers) if 0 <= i + by < peers]
    return lax.ppermute(value, axis, pairs)


def placed(first_row, row_count, doc_ends):
    position = first_row + jnp.arange(row_count, dtype=jnp.int32)
    segment = jnp.sum((position[:, None] >= doc_ends[None, :]).astype(jnp.int32), axis=1)
    return (position, segment)


def allowed(query_pos, query_seg, key_pos, key_seg):
    return (
        (key_pos[None, :] <= query_pos[:, None])
        & (key_pos[None, :] >= 0)
        & (key_seg[None, :] == query_seg[:, None])
    )


def absorb(softmax_state, query_heads, key_block, value_block, visible, scaling):
    running, denominator, accumulated = softmax_state
    scores = (
        jnp.einsum("bkgd,tkd->bkgt", query_heads, key_block, preferred_element_type=jnp.float32)
        * scaling
    )
    spread = visible[:, None, None, :]
    scores = jnp.where(spread, scores, -1e30)
    newest = jnp.maximum(running, jnp.max(scores, axis=-1))
    weight = jnp.where(spread, jnp.exp(scores - newest[..., None]), 0.0)
    shrink = jnp.exp(running - newest)
    denominator = denominator * shrink + jnp.sum(weight, axis=-1)
    accumulated = accumulated * shrink[..., None] + jnp.einsum(
        "bkgt,tkd->bkgd",
        weight.astype(jnp.bfloat16),
        value_block,
        preferred_element_type=jnp.float32,
    )
    return (newest, denominator, accumulated)


def contrib(query_heads, grad_heads, log_total, row_dot, key_block, value_block, visible, scaling):
    scores = (
        jnp.einsum("bkgd,tkd->bkgt", query_heads, key_block, preferred_element_type=jnp.float32)
        * scaling
    )
    spread = visible[:, None, None, :]
    scores = jnp.where(spread, scores, -1e30)
    probability = jnp.where(spread, jnp.exp(scores - log_total[..., None]), 0.0)
    value_part = jnp.einsum(
        "bkgt,bkgd->tkd",
        probability.astype(jnp.bfloat16),
        grad_heads,
        preferred_element_type=jnp.float32,
    )
    grad_prob = jnp.einsum(
        "bkgd,tkd->bkgt", grad_heads, value_block, preferred_element_type=jnp.float32
    )
    grad_score = (probability * (grad_prob - row_dot[..., None])).astype(jnp.bfloat16)
    query_part = (
        jnp.einsum("bkgt,tkd->bkgd", grad_score, key_block, preferred_element_type=jnp.float32)
        * scaling
    )
    key_part = (
        jnp.einsum("bkgt,bkgd->tkd", grad_score, query_heads, preferred_element_type=jnp.float32)
        * scaling
    )
    return (query_part, key_part, value_part)


def to_heads(arrays, groups):
    rows = arrays[0].shape[0]
    widths = [a.shape[1] // groups for a in arrays]
    joined = jnp.concatenate([a.reshape(rows, groups, -1) for a in arrays], axis=2)
    moved = lax.all_to_all(joined, "tp", split_axis=1, concat_axis=0, tiled=True)
    moved = moved.reshape(rows * groups, -1)
    pieces = []
    start = 0
    for w in widths:
        pieces.append(moved[:, start:start + w])
        start += w
    return pieces


def from_heads(arrays, groups):
    rows = arrays[0].shape[0] // groups
    widths = [a.shape[1] for a in arrays]
    joined = jnp.concatenate(arrays, axis=1).reshape(groups, rows, 1, -1)
    moved = lax.all_to_all(joined, "tp", split_axis=0, concat_axis=2, tiled=True)
    moved = moved.reshape(rows, groups, -1)
    pieces = []
    start = 0
    for w in widths:
        pieces.append(moved[:, :, start:start + w].reshape(rows, groups * w))
        start += w
    return pieces


def per_device(query_rows, key_rows, value_rows, out_grad, doc_lengths):
    per_kv = QH // KVH
    scaling = HD ** (-0.5)
    groups = lax.axis_size("tp")
    query_here, key_here, value_here = to_heads([query_rows, key_rows, value_rows], groups)
    (grad_here,) = to_heads([out_grad], groups)
    length = query_here.shape[0]
    kv_heads = key_here.shape[1] // HD
    query_heads = query_here.reshape(length, kv_heads, per_kv, HD)
    grad_heads = grad_here.reshape(length, kv_heads, per_kv, HD)
    seq_count = lax.axis_size("seq")
    position = lax.axis_index("seq")
    doc_ends = jnp.cumsum(doc_lengths)
    first_query = position * length
    query_pos, query_seg = placed(first_query, length, doc_ends)
    reach = min((length - 1 + LONG - 1) // length, seq_count - 1)

    key_value = jnp.stack((key_here, value_here))
    gathered = [key_value]
    depth = [0]
    while len(gathered) < reach + 1:
        step = len(gathered)
        take = min(step, reach + 1 - step)
        arrived = shifted(jnp.stack(gathered[:take]), "seq", step)
        gathered += [arrived[i] for i in range(take)]
        depth += [1 + max(depth[:take])] * take
    order = sorted(range(reach + 1), key=lambda d: (depth[d], d))

    doc_start = jnp.max(
        jnp.where(doc_ends[None, :] <= query_pos[:, None], doc_ends[None, :], 0), axis=1
    )

    def block_mask(d):
        key_pos = first_query - d * length + jnp.arange(length, dtype=jnp.int32)
        return (key_pos[None, :] >= doc_start[:, None]) & (key_pos[None, :] <= query_pos[:, None])

    softmax_state = (
        jnp.full((length, kv_heads, per_kv), -1e30, jnp.float32),
        jnp.zeros((length, kv_heads, per_kv), jnp.float32),
        jnp.zeros((length, kv_heads, per_kv, HD), jnp.float32),
    )
    for d in order:
        softmax_state, block = lax.optimization_barrier((softmax_state, gathered[d]))
        key_block = block[0].reshape(length, kv_heads, HD)
        value_block = block[1].reshape(length, kv_heads, HD)
        softmax_state = absorb(
            softmax_state, query_heads, key_block, value_block, block_mask(d), scaling
        )
    running, denominator, accumulated = softmax_state
    out_heads = (accumulated / denominator[..., None]).astype(jnp.bfloat16)
    log_total = running + jnp.log(denominator)
    row_dot = jnp.sum(grad_heads.astype(jnp.float32) * out_heads.astype(jnp.float32), axis=-1)

    query_acc = jnp.zeros((length, kv_heads, per_kv, HD), jnp.float32)
    sent = {}
    for d in range(reach, -1, -1):
        arrived = sent.pop(d + 3, None)
        if arrived is None:
            query_acc, block = lax.optimization_barrier((query_acc, gathered[d]))
        else:
            query_acc, block, arrived = lax.optimization_barrier((query_acc, gathered[d], arrived))
            sent[("in", d + 3)] = arrived
        key_block = block[0].reshape(length, kv_heads, HD)
        value_block = block[1].reshape(length, kv_heads, HD)
        query_part, key_part, value_part = contrib(
            query_heads, grad_heads, log_total, row_dot, key_block, value_block,
            block_mask(d), scaling,
        )
        query_acc = query_acc + query_part
        part = jnp.stack((key_part.reshape(length, -1), value_part.reshape(length, -1)))
        if d > 0:
            sent[d] = shifted(part.astype(jnp.bfloat16), "seq", -d)
        else:
            own = part
    grad_sums = own
    for received in sent.values():
        grad_sums = grad_sums + received.astype(jnp.float32)

    return tuple(
        from_heads(
            [
                out_heads.reshape(length, -1),
                query_acc.astype(jnp.bfloat16).reshape(length, -1),
                grad_sums[0].astype(jnp.bfloat16),
                grad_sums[1].astype(jnp.bfloat16),
            ],
            groups,
        )
    )


def solution(mesh):
    return jax.shard_map(
        per_device,
        mesh=mesh,
        in_specs=(
            P(("seq", "tp"), None),
            P(("seq", "tp"), None),
            P(("seq", "tp"), None),
            P(("seq", "tp"), None),
            P(),
        ),
        out_specs=(
            P(("seq", "tp"), None),
            P(("seq", "tp"), None),
            P(("seq", "tp"), None),
            P(("seq", "tp"), None),
        ),
        check_vma=False,
    )
```

```python
import jax
import jax.numpy as jnp
from jax import lax
from jax.sharding import PartitionSpec as P

HD = 128
QH = 20
KVH = 4
LONG = 4096


def shifted(value, axis, by):
    peers = lax.axis_size(axis)
    pairs = [(i, i + by) for i in range(peers) if 0 <= i + by < peers]
    return lax.ppermute(value, axis, pairs)


def placed(first_row, row_count, doc_ends):
    position = first_row + jnp.arange(row_count, dtype=jnp.int32)
    segment = jnp.sum((position[:, None] >= doc_ends[None, :]).astype(jnp.int32), axis=1)
    return (position, segment)


def allowed(query_pos, query_seg, key_pos, key_seg):
    return (
        (key_pos[None, :] <= query_pos[:, None])
        & (key_pos[None, :] >= 0)
        & (key_seg[None, :] == query_seg[:, None])
    )


def absorb(softmax_state, query_heads, key_block, value_block, visible, scaling):
    running, denominator, accumulated = softmax_state
    scores = (
        jnp.einsum("bkgd,tkd->bkgt", query_heads, key_block, preferred_element_type=jnp.float32)
        * scaling
    )
    spread = visible[:, None, None, :]
    scores = jnp.where(spread, scores, -1e30)
    newest = jnp.maximum(running, jnp.max(scores, axis=-1))
    weight = jnp.where(spread, jnp.exp(scores - newest[..., None]), 0.0)
    shrink = jnp.exp(running - newest)
    denominator = denominator * shrink + jnp.sum(weight, axis=-1)
    accumulated = accumulated * shrink[..., None] + jnp.einsum(
        "bkgt,tkd->bkgd",
        weight.astype(jnp.bfloat16),
        value_block,
        preferred_element_type=jnp.float32,
    )
    return (newest, denominator, accumulated)


def contrib(query_heads, grad_heads, log_total, row_dot, key_block, value_block, visible, scaling):
    scores = (
        jnp.einsum("bkgd,tkd->bkgt", query_heads, key_block, preferred_element_type=jnp.float32)
        * scaling
    )
    spread = visible[:, None, None, :]
    scores = jnp.where(spread, scores, -1e30)
    probability = jnp.where(spread, jnp.exp(scores - log_total[..., None]), 0.0)
    value_part = jnp.einsum(
        "bkgt,bkgd->tkd",
        probability.astype(jnp.bfloat16),
        grad_heads,
        preferred_element_type=jnp.float32,
    )
    grad_prob = jnp.einsum(
        "bkgd,tkd->bkgt", grad_heads, value_block, preferred_element_type=jnp.float32
    )
    grad_score = (probability * (grad_prob - row_dot[..., None])).astype(jnp.bfloat16)
    query_part = (
        jnp.einsum("bkgt,tkd->bkgd", grad_score, key_block, preferred_element_type=jnp.float32)
        * scaling
    )
    key_part = (
        jnp.einsum("bkgt,bkgd->tkd", grad_score, query_heads, preferred_element_type=jnp.float32)
        * scaling
    )
    return (query_part, key_part, value_part)


def to_heads(arrays, groups):
    rows = arrays[0].shape[0]
    widths = [a.shape[1] // groups for a in arrays]
    joined = jnp.concatenate([a.reshape(rows, groups, -1) for a in arrays], axis=2)
    moved = lax.all_to_all(joined, "tp", split_axis=1, concat_axis=0, tiled=True)
    moved = moved.reshape(rows * groups, -1)
    pieces = []
    start = 0
    for w in widths:
        pieces.append(moved[:, start:start + w])
        start += w
    return pieces


def from_heads(arrays, groups):
    rows = arrays[0].shape[0] // groups
    widths = [a.shape[1] for a in arrays]
    joined = jnp.concatenate(arrays, axis=1).reshape(groups, rows, 1, -1)
    moved = lax.all_to_all(joined, "tp", split_axis=0, concat_axis=2, tiled=True)
    moved = moved.reshape(rows, groups, -1)
    pieces = []
    start = 0
    for w in widths:
        pieces.append(moved[:, :, start:start + w].reshape(rows, groups * w))
        start += w
    return pieces


def per_device(query_rows, key_rows, value_rows, out_grad, doc_lengths):
    per_kv = QH // KVH
    scaling = HD ** (-0.5)
    groups = lax.axis_size("tp")
    query_here, key_here, value_here = to_heads([query_rows, key_rows, value_rows], groups)
    length = query_here.shape[0]
    kv_heads = key_here.shape[1] // HD
    query_heads = query_here.reshape(length, kv_heads, per_kv, HD)
    seq_count = lax.axis_size("seq")
    position = lax.axis_index("seq")
    doc_ends = jnp.cumsum(doc_lengths)
    first_query = position * length
    query_pos, query_seg = placed(first_query, length, doc_ends)
    reach = min((length - 1 + LONG - 1) // length, seq_count - 1)

    key_value = jnp.stack((key_here, value_here))
    gathered = [key_value]
    depth = [0]
    while len(gathered) < reach + 1:
        step = len(gathered)
        take = min(step, reach + 1 - step)
        arrived = shifted(jnp.stack(gathered[:take]), "seq", step)
        gathered += [arrived[i] for i in range(take)]
        depth += [1 + max(depth[:take])] * take
    order = sorted(range(reach + 1), key=lambda d: (depth[d], d))

    doc_start = jnp.max(
        jnp.where(doc_ends[None, :] <= query_pos[:, None], doc_ends[None, :], 0), axis=1
    )

    def block_mask(d):
        key_pos = first_query - d * length + jnp.arange(length, dtype=jnp.int32)
        return (key_pos[None, :] >= doc_start[:, None]) & (key_pos[None, :] <= query_pos[:, None])

    softmax_state = (
        jnp.full((length, kv_heads, per_kv), -1e30, jnp.float32),
        jnp.zeros((length, kv_heads, per_kv), jnp.float32),
        jnp.zeros((length, kv_heads, per_kv, HD), jnp.float32),
    )
    for d in order:
        softmax_state, block = lax.optimization_barrier((softmax_state, gathered[d]))
        key_block = block[0].reshape(length, kv_heads, HD)
        value_block = block[1].reshape(length, kv_heads, HD)
        softmax_state = absorb(
            softmax_state, query_heads, key_block, value_block, block_mask(d), scaling
        )
        if d == 0:
            out_grad, softmax_state = lax.optimization_barrier((out_grad, softmax_state))
            (grad_here,) = to_heads([out_grad], groups)
            grad_heads = grad_here.reshape(length, kv_heads, per_kv, HD)
    running, denominator, accumulated = softmax_state
    out_heads = (accumulated / denominator[..., None]).astype(jnp.bfloat16)
    log_total = running + jnp.log(denominator)
    row_dot = jnp.sum(grad_heads.astype(jnp.float32) * out_heads.astype(jnp.float32), axis=-1)

    query_acc = jnp.zeros((length, kv_heads, per_kv, HD), jnp.float32)
    sent = {}
    for d in range(reach, -1, -1):
        arrived = sent.pop(d + 3, None)
        if arrived is None:
            query_acc, block = lax.optimization_barrier((query_acc, gathered[d]))
        else:
            query_acc, block, arrived = lax.optimization_barrier((query_acc, gathered[d], arrived))
            sent[("in", d + 3)] = arrived
        key_block = block[0].reshape(length, kv_heads, HD)
        value_block = block[1].reshape(length, kv_heads, HD)
        query_part, key_part, value_part = contrib(
            query_heads, grad_heads, log_total, row_dot, key_block, value_block,
            block_mask(d), scaling,
        )
        query_acc = query_acc + query_part
        part = jnp.stack((key_part.reshape(length, -1), value_part.reshape(length, -1)))
        if d > 0:
            sent[d] = shifted(part.astype(jnp.bfloat16), "seq", -d)
        else:
            own = part
    grad_sums = own
    for received in sent.values():
        grad_sums = grad_sums + received.astype(jnp.float32)

    return tuple(
        from_heads(
            [
                out_heads.reshape(length, -1),
                query_acc.astype(jnp.bfloat16).reshape(length, -1),
                grad_sums[0].astype(jnp.bfloat16),
                grad_sums[1].astype(jnp.bfloat16),
            ],
            groups,
        )
    )


def solution(mesh):
    return jax.shard_map(
        per_device,
        mesh=mesh,
        in_specs=(
            P(("seq", "tp"), None),
            P(("seq", "tp"), None),
            P(("seq", "tp"), None),
            P(("seq", "tp"), None),
            P(),
        ),
        out_specs=(
            P(("seq", "tp"), None),
            P(("seq", "tp"), None),
            P(("seq", "tp"), None),
            P(("seq", "tp"), None),
        ),
        check_vma=False,
    )
```

```python
import jax
import jax.numpy as jnp
from jax import lax
from jax.sharding import PartitionSpec as P

HD = 128
QH = 20
KVH = 4
LONG = 4096


def shifted(value, axis, by):
    peers = lax.axis_size(axis)
    pairs = [(i, i + by) for i in range(peers) if 0 <= i + by < peers]
    return lax.ppermute(value, axis, pairs)


def placed(first_row, row_count, doc_ends):
    position = first_row + jnp.arange(row_count, dtype=jnp.int32)
    segment = jnp.sum((position[:, None] >= doc_ends[None, :]).astype(jnp.int32), axis=1)
    return (position, segment)


def allowed(query_pos, query_seg, key_pos, key_seg):
    return (
        (key_pos[None, :] <= query_pos[:, None])
        & (key_pos[None, :] >= 0)
        & (key_seg[None, :] == query_seg[:, None])
    )


def absorb(softmax_state, query_heads, key_block, value_block, visible, scaling):
    running, denominator, accumulated = softmax_state
    scores = (
        jnp.einsum("bkgd,tkd->bkgt", query_heads, key_block, preferred_element_type=jnp.float32)
        * scaling
    )
    spread = visible[:, None, None, :]
    scores = jnp.where(spread, scores, -1e30)
    newest = jnp.maximum(running, jnp.max(scores, axis=-1))
    weight = jnp.where(spread, jnp.exp(scores - newest[..., None]), 0.0)
    shrink = jnp.exp(running - newest)
    denominator = denominator * shrink + jnp.sum(weight, axis=-1)
    accumulated = accumulated * shrink[..., None] + jnp.einsum(
        "bkgt,tkd->bkgd",
        weight.astype(jnp.bfloat16),
        value_block,
        preferred_element_type=jnp.float32,
    )
    return (newest, denominator, accumulated)


def contrib(query_heads, grad_heads, log_total, row_dot, key_block, value_block, visible, scaling):
    scores = (
        jnp.einsum("bkgd,tkd->bkgt", query_heads, key_block, preferred_element_type=jnp.float32)
        * scaling
    )
    spread = visible[:, None, None, :]
    scores = jnp.where(spread, scores, -1e30)
    probability = jnp.where(spread, jnp.exp(scores - log_total[..., None]), 0.0)
    value_part = jnp.einsum(
        "bkgt,bkgd->tkd",
        probability.astype(jnp.bfloat16),
        grad_heads,
        preferred_element_type=jnp.float32,
    )
    grad_prob = jnp.einsum(
        "bkgd,tkd->bkgt", grad_heads, value_block, preferred_element_type=jnp.float32
    )
    grad_score = (probability * (grad_prob - row_dot[..., None])).astype(jnp.bfloat16)
    query_part = (
        jnp.einsum("bkgt,tkd->bkgd", grad_score, key_block, preferred_element_type=jnp.float32)
        * scaling
    )
    key_part = (
        jnp.einsum("bkgt,bkgd->tkd", grad_score, query_heads, preferred_element_type=jnp.float32)
        * scaling
    )
    return (query_part, key_part, value_part)


def to_heads(arrays, groups):
    rows = arrays[0].shape[0]
    widths = [a.shape[1] // groups for a in arrays]
    joined = jnp.concatenate([a.reshape(rows, groups, -1) for a in arrays], axis=2)
    moved = lax.all_to_all(joined, "tp", split_axis=1, concat_axis=0, tiled=True)
    moved = moved.reshape(rows * groups, -1)
    pieces = []
    start = 0
    for w in widths:
        pieces.append(moved[:, start:start + w])
        start += w
    return pieces


def from_heads(arrays, groups):
    rows = arrays[0].shape[0] // groups
    widths = [a.shape[1] for a in arrays]
    joined = jnp.concatenate(arrays, axis=1).reshape(groups, rows, 1, -1)
    moved = lax.all_to_all(joined, "tp", split_axis=0, concat_axis=2, tiled=True)
    moved = moved.reshape(rows, groups, -1)
    pieces = []
    start = 0
    for w in widths:
        pieces.append(moved[:, :, start:start + w].reshape(rows, groups * w))
        start += w
    return pieces


def per_device(query_rows, key_rows, value_rows, out_grad, doc_lengths):
    per_kv = QH // KVH
    scaling = HD ** (-0.5)
    groups = lax.axis_size("tp")
    query_here, key_here, value_here = to_heads([query_rows, key_rows, value_rows], groups)
    (grad_here,) = to_heads([out_grad], groups)
    length = query_here.shape[0]
    kv_heads = key_here.shape[1] // HD
    query_heads = query_here.reshape(length, kv_heads, per_kv, HD)
    grad_heads = grad_here.reshape(length, kv_heads, per_kv, HD)
    seq_count = lax.axis_size("seq")
    position = lax.axis_index("seq")
    doc_ends = jnp.cumsum(doc_lengths)
    first_query = position * length
    query_pos, query_seg = placed(first_query, length, doc_ends)
    reach = min((length - 1 + LONG - 1) // length, seq_count - 1)

    key_value = jnp.stack((key_here, value_here))
    gathered = [key_value]
    depth = [0]
    while len(gathered) < reach + 1:
        step = len(gathered)
        take = min(step, reach + 1 - step)
        for first in range(0, take, 2):
            sources = list(range(first, min(first + 2, take)))
            arrived = shifted(jnp.stack([gathered[j] for j in sources]), "seq", step)
            gathered += [arrived[i] for i in range(len(sources))]
            depth += [1 + max(depth[j] for j in sources)] * len(sources)
    order = sorted(range(reach + 1), key=lambda d: (depth[d], d))

    doc_start = jnp.max(
        jnp.where(doc_ends[None, :] <= query_pos[:, None], doc_ends[None, :], 0), axis=1
    )

    def block_mask(d):
        key_pos = first_query - d * length + jnp.arange(length, dtype=jnp.int32)
        return (key_pos[None, :] >= doc_start[:, None]) & (key_pos[None, :] <= query_pos[:, None])

    softmax_state = (
        jnp.full((length, kv_heads, per_kv), -1e30, jnp.float32),
        jnp.zeros((length, kv_heads, per_kv), jnp.float32),
        jnp.zeros((length, kv_heads, per_kv, HD), jnp.float32),
    )
    for d in order:
        softmax_state, block = lax.optimization_barrier((softmax_state, gathered[d]))
        key_block = block[0].reshape(length, kv_heads, HD)
        value_block = block[1].reshape(length, kv_heads, HD)
        softmax_state = absorb(
            softmax_state, query_heads, key_block, value_block, block_mask(d), scaling
        )
    running, denominator, accumulated = softmax_state
    out_heads = (accumulated / denominator[..., None]).astype(jnp.bfloat16)
    log_total = running + jnp.log(denominator)
    row_dot = jnp.sum(grad_heads.astype(jnp.float32) * out_heads.astype(jnp.float32), axis=-1)

    query_acc = jnp.zeros((length, kv_heads, per_kv, HD), jnp.float32)
    sent = {}
    for d in range(reach, -1, -1):
        arrived = sent.pop(d + 3, None)
        if arrived is None:
            query_acc, block = lax.optimization_barrier((query_acc, gathered[d]))
        else:
            query_acc, block, arrived = lax.optimization_barrier((query_acc, gathered[d], arrived))
            sent[("in", d + 3)] = arrived
        key_block = block[0].reshape(length, kv_heads, HD)
        value_block = block[1].reshape(length, kv_heads, HD)
        query_part, key_part, value_part = contrib(
            query_heads, grad_heads, log_total, row_dot, key_block, value_block,
            block_mask(d), scaling,
        )
        query_acc = query_acc + query_part
        part = jnp.stack((key_part.reshape(length, -1), value_part.reshape(length, -1)))
        if d > 0:
            sent[d] = shifted(part.astype(jnp.bfloat16), "seq", -d)
        else:
            own = part
    grad_sums = own
    for received in sent.values():
        grad_sums = grad_sums + received.astype(jnp.float32)

    return tuple(
        from_heads(
            [
                out_heads.reshape(length, -1),
                query_acc.astype(jnp.bfloat16).reshape(length, -1),
                grad_sums[0].astype(jnp.bfloat16),
                grad_sums[1].astype(jnp.bfloat16),
            ],
            groups,
        )
    )


def solution(mesh):
    return jax.shard_map(
        per_device,
        mesh=mesh,
        in_specs=(
            P(("seq", "tp"), None),
            P(("seq", "tp"), None),
            P(("seq", "tp"), None),
            P(("seq", "tp"), None),
            P(),
        ),
        out_specs=(
            P(("seq", "tp"), None),
            P(("seq", "tp"), None),
            P(("seq", "tp"), None),
            P(("seq", "tp"), None),
        ),
        check_vma=False,
    )
```

```python
import jax
import jax.numpy as jnp
from jax import lax
from jax.sharding import PartitionSpec as P

HD = 128
QH = 20
KVH = 4
LONG = 4096


def shifted(value, axis, by):
    peers = lax.axis_size(axis)
    pairs = [(i, i + by) for i in range(peers) if 0 <= i + by < peers]
    return lax.ppermute(value, axis, pairs)


def placed(first_row, row_count, doc_ends):
    position = first_row + jnp.arange(row_count, dtype=jnp.int32)
    segment = jnp.sum((position[:, None] >= doc_ends[None, :]).astype(jnp.int32), axis=1)
    return (position, segment)


def allowed(query_pos, query_seg, key_pos, key_seg):
    return (
        (key_pos[None, :] <= query_pos[:, None])
        & (key_pos[None, :] >= 0)
        & (key_seg[None, :] == query_seg[:, None])
    )


def absorb(softmax_state, query_heads, key_block, value_block, visible, scaling):
    running, denominator, accumulated = softmax_state
    scores = (
        jnp.einsum("bkgd,tkd->bkgt", query_heads, key_block, preferred_element_type=jnp.float32)
        * scaling
    )
    spread = visible[:, None, None, :]
    scores = jnp.where(spread, scores, -1e30)
    newest = jnp.maximum(running, jnp.max(scores, axis=-1))
    weight = jnp.where(spread, jnp.exp(scores - newest[..., None]), 0.0)
    shrink = jnp.exp(running - newest)
    denominator = denominator * shrink + jnp.sum(weight, axis=-1)
    accumulated = accumulated * shrink[..., None] + jnp.einsum(
        "bkgt,tkd->bkgd",
        weight.astype(jnp.bfloat16),
        value_block,
        preferred_element_type=jnp.float32,
    )
    return (newest, denominator, accumulated)


def contrib(query_heads, grad_heads, log_total, row_dot, key_block, value_block, visible, scaling):
    scores = (
        jnp.einsum("bkgd,tkd->bkgt", query_heads, key_block, preferred_element_type=jnp.float32)
        * scaling
    )
    spread = visible[:, None, None, :]
    scores = jnp.where(spread, scores, -1e30)
    probability = jnp.where(spread, jnp.exp(scores - log_total[..., None]), 0.0)
    value_part = jnp.einsum(
        "bkgt,bkgd->tkd",
        probability.astype(jnp.bfloat16),
        grad_heads,
        preferred_element_type=jnp.float32,
    )
    grad_prob = jnp.einsum(
        "bkgd,tkd->bkgt", grad_heads, value_block, preferred_element_type=jnp.float32
    )
    grad_score = (probability * (grad_prob - row_dot[..., None])).astype(jnp.bfloat16)
    query_part = (
        jnp.einsum("bkgt,tkd->bkgd", grad_score, key_block, preferred_element_type=jnp.float32)
        * scaling
    )
    key_part = (
        jnp.einsum("bkgt,bkgd->tkd", grad_score, query_heads, preferred_element_type=jnp.float32)
        * scaling
    )
    return (query_part, key_part, value_part)


def to_heads(arrays, groups):
    rows = arrays[0].shape[0]
    widths = [a.shape[1] // groups for a in arrays]
    joined = jnp.concatenate([a.reshape(rows, groups, -1) for a in arrays], axis=2)
    moved = lax.all_to_all(joined, "tp", split_axis=1, concat_axis=0, tiled=True)
    moved = moved.reshape(rows * groups, -1)
    pieces = []
    start = 0
    for w in widths:
        pieces.append(moved[:, start:start + w])
        start += w
    return pieces


def from_heads(arrays, groups):
    rows = arrays[0].shape[0] // groups
    widths = [a.shape[1] for a in arrays]
    joined = jnp.concatenate(arrays, axis=1).reshape(groups, rows, 1, -1)
    moved = lax.all_to_all(joined, "tp", split_axis=0, concat_axis=2, tiled=True)
    moved = moved.reshape(rows, groups, -1)
    pieces = []
    start = 0
    for w in widths:
        pieces.append(moved[:, :, start:start + w].reshape(rows, groups * w))
        start += w
    return pieces


def per_device(query_rows, key_rows, value_rows, out_grad, doc_lengths):
    per_kv = QH // KVH
    scaling = HD ** (-0.5)
    groups = lax.axis_size("tp")
    query_here, key_here, value_here = to_heads([query_rows, key_rows, value_rows], groups)
    (grad_here,) = to_heads([out_grad], groups)
    length = query_here.shape[0]
    kv_heads = key_here.shape[1] // HD
    query_heads = query_here.reshape(length, kv_heads, per_kv, HD)
    grad_heads = grad_here.reshape(length, kv_heads, per_kv, HD)
    seq_count = lax.axis_size("seq")
    position = lax.axis_index("seq")
    doc_ends = jnp.cumsum(doc_lengths)
    first_query = position * length
    query_pos, query_seg = placed(first_query, length, doc_ends)
    reach = min((length - 1 + LONG - 1) // length, seq_count - 1)

    key_value = jnp.stack((key_here, value_here))
    gathered = [key_value]
    depth = [0]
    while len(gathered) < reach + 1:
        step = len(gathered)
        take = min(step, reach + 1 - step)
        arrived = shifted(jnp.stack(gathered[:take]), "seq", step)
        gathered += [arrived[i] for i in range(take)]
        depth += [1 + max(depth[:take])] * take
    order = sorted(range(reach + 1), key=lambda d: (depth[d], -d))

    doc_start = jnp.max(
        jnp.where(doc_ends[None, :] <= query_pos[:, None], doc_ends[None, :], 0), axis=1
    )

    def block_mask(d):
        key_pos = first_query - d * length + jnp.arange(length, dtype=jnp.int32)
        return (key_pos[None, :] >= doc_start[:, None]) & (key_pos[None, :] <= query_pos[:, None])

    softmax_state = (
        jnp.full((length, kv_heads, per_kv), -1e30, jnp.float32),
        jnp.zeros((length, kv_heads, per_kv), jnp.float32),
        jnp.zeros((length, kv_heads, per_kv, HD), jnp.float32),
    )
    for d in order:
        softmax_state, block = lax.optimization_barrier((softmax_state, gathered[d]))
        key_block = block[0].reshape(length, kv_heads, HD)
        value_block = block[1].reshape(length, kv_heads, HD)
        softmax_state = absorb(
            softmax_state, query_heads, key_block, value_block, block_mask(d), scaling
        )
    running, denominator, accumulated = softmax_state
    out_heads = (accumulated / denominator[..., None]).astype(jnp.bfloat16)
    log_total = running + jnp.log(denominator)
    row_dot = jnp.sum(grad_heads.astype(jnp.float32) * out_heads.astype(jnp.float32), axis=-1)

    query_acc = jnp.zeros((length, kv_heads, per_kv, HD), jnp.float32)
    sent = {}
    for d in range(reach, -1, -1):
        arrived = sent.pop(d + 3, None)
        if arrived is None:
            query_acc, block = lax.optimization_barrier((query_acc, gathered[d]))
        else:
            query_acc, block, arrived = lax.optimization_barrier((query_acc, gathered[d], arrived))
            sent[("in", d + 3)] = arrived
        key_block = block[0].reshape(length, kv_heads, HD)
        value_block = block[1].reshape(length, kv_heads, HD)
        query_part, key_part, value_part = contrib(
            query_heads, grad_heads, log_total, row_dot, key_block, value_block,
            block_mask(d), scaling,
        )
        query_acc = query_acc + query_part
        part = jnp.stack((key_part.reshape(length, -1), value_part.reshape(length, -1)))
        if d > 0:
            sent[d] = shifted(part.astype(jnp.bfloat16), "seq", -d)
        else:
            own = part
    grad_sums = own
    for received in sent.values():
        grad_sums = grad_sums + received.astype(jnp.float32)

    return tuple(
        from_heads(
            [
                out_heads.reshape(length, -1),
                query_acc.astype(jnp.bfloat16).reshape(length, -1),
                grad_sums[0].astype(jnp.bfloat16),
                grad_sums[1].astype(jnp.bfloat16),
            ],
            groups,
        )
    )


def solution(mesh):
    return jax.shard_map(
        per_device,
        mesh=mesh,
        in_specs=(
            P(("seq", "tp"), None),
            P(("seq", "tp"), None),
            P(("seq", "tp"), None),
            P(("seq", "tp"), None),
            P(),
        ),
        out_specs=(
            P(("seq", "tp"), None),
            P(("seq", "tp"), None),
            P(("seq", "tp"), None),
            P(("seq", "tp"), None),
        ),
        check_vma=False,
    )
```

```python
import jax
import jax.numpy as jnp
from jax import lax
from jax.sharding import PartitionSpec as P

HD = 128
QH = 20
KVH = 4
LONG = 4096


def shifted(value, axis, by):
    peers = lax.axis_size(axis)
    pairs = [(i, i + by) for i in range(peers) if 0 <= i + by < peers]
    return lax.ppermute(value, axis, pairs)


def placed(first_row, row_count, doc_ends):
    position = first_row + jnp.arange(row_count, dtype=jnp.int32)
    segment = jnp.sum((position[:, None] >= doc_ends[None, :]).astype(jnp.int32), axis=1)
    return (position, segment)


def allowed(query_pos, query_seg, key_pos, key_seg):
    return (
        (key_pos[None, :] <= query_pos[:, None])
        & (key_pos[None, :] >= 0)
        & (key_seg[None, :] == query_seg[:, None])
    )


def absorb(softmax_state, query_heads, key_block, value_block, visible, scaling):
    running, denominator, accumulated = softmax_state
    scores = (
        jnp.einsum("bkgd,tkd->bkgt", query_heads, key_block, preferred_element_type=jnp.float32)
        * scaling
    )
    spread = visible[:, None, None, :]
    scores = jnp.where(spread, scores, -1e30)
    newest = jnp.maximum(running, jnp.max(scores, axis=-1))
    weight = jnp.where(spread, jnp.exp(scores - newest[..., None]), 0.0)
    shrink = jnp.exp(running - newest)
    denominator = denominator * shrink + jnp.sum(weight, axis=-1)
    accumulated = accumulated * shrink[..., None] + jnp.einsum(
        "bkgt,tkd->bkgd",
        weight.astype(jnp.bfloat16),
        value_block,
        preferred_element_type=jnp.float32,
    )
    return (newest, denominator, accumulated)


def contrib(query_heads, grad_heads, log_total, row_dot, key_block, value_block, visible, scaling):
    scores = (
        jnp.einsum("bkgd,tkd->bkgt", query_heads, key_block, preferred_element_type=jnp.float32)
        * scaling
    )
    spread = visible[:, None, None, :]
    scores = jnp.where(spread, scores, -1e30)
    probability = jnp.where(spread, jnp.exp(scores - log_total[..., None]), 0.0)
    value_part = jnp.einsum(
        "bkgt,bkgd->tkd",
        probability.astype(jnp.bfloat16),
        grad_heads,
        preferred_element_type=jnp.float32,
    )
    grad_prob = jnp.einsum(
        "bkgd,tkd->bkgt", grad_heads, value_block, preferred_element_type=jnp.float32
    )
    grad_score = (probability * (grad_prob - row_dot[..., None])).astype(jnp.bfloat16)
    query_part = (
        jnp.einsum("bkgt,tkd->bkgd", grad_score, key_block, preferred_element_type=jnp.float32)
        * scaling
    )
    key_part = (
        jnp.einsum("bkgt,bkgd->tkd", grad_score, query_heads, preferred_element_type=jnp.float32)
        * scaling
    )
    return (query_part, key_part, value_part)


def to_heads(arrays, groups):
    rows = arrays[0].shape[0]
    widths = [a.shape[1] // groups for a in arrays]
    joined = jnp.concatenate([a.reshape(rows, groups, -1) for a in arrays], axis=2)
    moved = lax.all_to_all(joined, "tp", split_axis=1, concat_axis=0, tiled=True)
    moved = moved.reshape(rows * groups, -1)
    pieces = []
    start = 0
    for w in widths:
        pieces.append(moved[:, start:start + w])
        start += w
    return pieces


def from_heads(arrays, groups):
    rows = arrays[0].shape[0] // groups
    widths = [a.shape[1] for a in arrays]
    joined = jnp.concatenate(arrays, axis=1).reshape(groups, rows, 1, -1)
    moved = lax.all_to_all(joined, "tp", split_axis=0, concat_axis=2, tiled=True)
    moved = moved.reshape(rows, groups, -1)
    pieces = []
    start = 0
    for w in widths:
        pieces.append(moved[:, :, start:start + w].reshape(rows, groups * w))
        start += w
    return pieces


def per_device(query_rows, key_rows, value_rows, out_grad, doc_lengths):
    per_kv = QH // KVH
    scaling = HD ** (-0.5)
    groups = lax.axis_size("tp")
    query_here, key_here, value_here = to_heads([query_rows, key_rows, value_rows], groups)
    (grad_here,) = to_heads([out_grad], groups)
    length = query_here.shape[0]
    kv_heads = key_here.shape[1] // HD
    query_heads = query_here.reshape(length, kv_heads, per_kv, HD)
    grad_heads = grad_here.reshape(length, kv_heads, per_kv, HD)
    seq_count = lax.axis_size("seq")
    position = lax.axis_index("seq")
    doc_ends = jnp.cumsum(doc_lengths)
    first_query = position * length
    query_pos, query_seg = placed(first_query, length, doc_ends)
    reach = min((length - 1 + LONG - 1) // length, seq_count - 1)

    key_value = jnp.stack((key_here, value_here))
    gathered = [key_value]
    depth = [0]
    while len(gathered) < reach + 1:
        step = len(gathered)
        take = min(step, reach + 1 - step)
        arrived = shifted(jnp.stack(gathered[:take]), "seq", step)
        gathered += [arrived[i] for i in range(take)]
        depth += [1 + max(depth[:take])] * take
    order = sorted(range(reach + 1), key=lambda d: (depth[d], -d if depth[d] == 1 else d))

    doc_start = jnp.max(
        jnp.where(doc_ends[None, :] <= query_pos[:, None], doc_ends[None, :], 0), axis=1
    )

    def block_mask(d):
        key_pos = first_query - d * length + jnp.arange(length, dtype=jnp.int32)
        return (key_pos[None, :] >= doc_start[:, None]) & (key_pos[None, :] <= query_pos[:, None])

    softmax_state = (
        jnp.full((length, kv_heads, per_kv), -1e30, jnp.float32),
        jnp.zeros((length, kv_heads, per_kv), jnp.float32),
        jnp.zeros((length, kv_heads, per_kv, HD), jnp.float32),
    )
    for d in order:
        softmax_state, block = lax.optimization_barrier((softmax_state, gathered[d]))
        key_block = block[0].reshape(length, kv_heads, HD)
        value_block = block[1].reshape(length, kv_heads, HD)
        softmax_state = absorb(
            softmax_state, query_heads, key_block, value_block, block_mask(d), scaling
        )
    running, denominator, accumulated = softmax_state
    out_heads = (accumulated / denominator[..., None]).astype(jnp.bfloat16)
    log_total = running + jnp.log(denominator)
    row_dot = jnp.sum(grad_heads.astype(jnp.float32) * out_heads.astype(jnp.float32), axis=-1)

    query_acc = jnp.zeros((length, kv_heads, per_kv, HD), jnp.float32)
    sent = {}
    for d in range(reach, -1, -1):
        arrived = sent.pop(d + 3, None)
        if arrived is None:
            query_acc, block = lax.optimization_barrier((query_acc, gathered[d]))
        else:
            query_acc, block, arrived = lax.optimization_barrier((query_acc, gathered[d], arrived))
            sent[("in", d + 3)] = arrived
        key_block = block[0].reshape(length, kv_heads, HD)
        value_block = block[1].reshape(length, kv_heads, HD)
        query_part, key_part, value_part = contrib(
            query_heads, grad_heads, log_total, row_dot, key_block, value_block,
            block_mask(d), scaling,
        )
        query_acc = query_acc + query_part
        part = jnp.stack((key_part.reshape(length, -1), value_part.reshape(length, -1)))
        if d > 0:
            sent[d] = shifted(part.astype(jnp.bfloat16), "seq", -d)
        else:
            own = part
    grad_sums = own
    for received in sent.values():
        grad_sums = grad_sums + received.astype(jnp.float32)

    return tuple(
        from_heads(
            [
                out_heads.reshape(length, -1),
                query_acc.astype(jnp.bfloat16).reshape(length, -1),
                grad_sums[0].astype(jnp.bfloat16),
                grad_sums[1].astype(jnp.bfloat16),
            ],
            groups,
        )
    )


def solution(mesh):
    return jax.shard_map(
        per_device,
        mesh=mesh,
        in_specs=(
            P(("seq", "tp"), None),
            P(("seq", "tp"), None),
            P(("seq", "tp"), None),
            P(("seq", "tp"), None),
            P(),
        ),
        out_specs=(
            P(("seq", "tp"), None),
            P(("seq", "tp"), None),
            P(("seq", "tp"), None),
            P(("seq", "tp"), None),
        ),
        check_vma=False,
    )
```
